32 devices in a mesh: groups: 2 (over y), ctx: 4 (over z), chan: 2 (over x), sub: 2 (over core).
Axes of the slice: x: 2, y: 2, z: 4, core: 2. Of those that a mesh axis runs over, the one named last changes fastest.
Arguments:
- queries: float32 [2048, 8192], P(('groups', 'ctx'), ('chan', 'sub')), parts along dimension 0, may hold values from -6 to 6
- key_in: float32 [2048, 8192], P(('groups', 'ctx'), ('chan', 'sub')), parts along dimension 0, may hold values from -6 to 6
- values_in: float32 [2048, 8192], P(('groups', 'ctx'), ('chan', 'sub')), parts along dimension 0, may hold values from -6 to 6
- skip_gain: float32 [8192], P(('chan', 'sub')), may hold values from 0.5 to 1.5
- filter_tap_bank: float32 [16, 256, 512], P(('ctx', 'sub'), None, 'chan'), may hold values from -0.1875 to 0.1875
- lag_slot: int32 [4], replicated, may hold values from 0 to 15, as said below
Outputs:
- gated_output: float32 [2048, 8192], P(('groups', 'ctx'), ('chan', 'sub')), parts along dimension 0
The draws below stay inside these ranges and needn't reach their ends.
There are 2 independent parts, one for each index of `groups`. The reference program is written for one: setup_inputs(seed, part) draws one part's arguments, and reference() takes and returns one part's arrays. A program takes and returns all parts, laid end to end along the dimension named above; an argument that names none is the same for every part. Nothing has to cross between parts.
Inputs may be any that keep to these rules, and one draw needn't show every extreme that they name: `lag_slot`: the 4 entries are distinct slots; entry k names the slot that holds lags k * 256 to (k + 1) * 256 - 1.
All inputs are finite; a program needn't handle non-finite values.
Results may differ from the reference program's by a relative error of at most 0.00005.
Values sent between devices are 32-bit elements; how exact they have to be, the bound alone decides.
No kernel may reach another device: no remote copies, remote signals or barrier semaphores. Data moves between devices by JAX's collectives and lax.ppermute only.
A program may use at most 128 MiB of HBM per device.

```python
import math
import jax
import jax.numpy as jnp
from jax import lax

CHANNELS = 8192
GROUP_CH = 16
SEGMENT_LENGTH = 256
SEGMENT_STEPS = 4
FILTER_GROUPS = 512
TOKENS = 1024
TOTAL_SLOTS = 16


def draw_lag_slot(key, part):
    first_key, second_key, key_order = jax.random.split(key, 3)
    first_choice = jax.random.randint(first_key, (), 1, TOTAL_SLOTS - 1)
    offset_choice = jax.random.randint(second_key, (), 1, TOTAL_SLOTS - 2)
    second_choice = 1 + (first_choice - 1 + offset_choice) % (TOTAL_SLOTS - 2)
    picked_slot = jnp.stack([jnp.int32(0), jnp.int32(TOTAL_SLOTS - 1), first_choice.astype(jnp.int32), second_choice.astype(jnp.int32)])
    return jax.random.permutation(key_order, picked_slot).astype(jnp.int32)


def block_scale(stream_key, shape, pieces, low, top_value):
    level, own = 1.0, jax.random.fold_in(stream_key, 6)
    for position, parts in pieces:
        draws = jnp.exp(jax.random.uniform(jax.random.fold_in(own, position), (parts,), jnp.float32, low / len(pieces), top_value / len(pieces)))
        level = level * jnp.repeat(draws, shape[position] // parts).reshape([-1 if axis == position else 1 for axis in range(len(shape))])
    return level


def noise(rng, dims, deviation, reach, shards=(), kind=jnp.bfloat16):
    result = deviation * jax.random.normal(rng, dims, jnp.float32)
    if shards:
        result = result * block_scale(rng, dims, shards, -0.22, 0.18)
    return jnp.clip(result, -reach, reach).astype(kind)


def setup_inputs(seed: int = 0, part: int = 0) -> dict:
    splits = jax.random.split(jax.random.key(seed), 7)
    part_keys = jax.random.split(jax.random.fold_in(splits[6], part), 7)
    queries = noise(part_keys[0], (TOKENS, CHANNELS), 1.0, 6.0, ((0, 4), (1, 4)), jnp.float32)
    key_in = noise(part_keys[1], (TOKENS, CHANNELS), 1.0, 6.0, ((0, 4), (1, 4)), jnp.float32)
    values_in = noise(part_keys[2], (TOKENS, CHANNELS), 1.0, 6.0, ((0, 4), (1, 4)), jnp.float32)
    skip_gain = jnp.clip(0.5 + 1.0 * jax.random.uniform(splits[3], (CHANNELS,), jnp.float32) ** block_scale(splits[3], (CHANNELS,), ((0, 4),), -0.2, 0.2), 0.5, 1.5)
    filter_tap_bank = noise(splits[4], (TOTAL_SLOTS, SEGMENT_LENGTH, FILTER_GROUPS), (SEGMENT_STEPS * SEGMENT_LENGTH) ** -0.5, 0.1875, ((0, 8), (2, 2)), jnp.float32)
    lag_slot = draw_lag_slot(jax.random.fold_in(splits[6], 71), part)
    return dict(queries=queries, key_in=key_in, values_in=values_in, skip_gain=skip_gain, filter_tap_bank=filter_tap_bank, lag_slot=lag_slot)


def reference(queries, key_in, values_in, skip_gain, filter_tap_bank, lag_slot):
    mixed = key_in * values_in
    filter_taps = jnp.concatenate([filter_tap_bank[lag_slot[cycle_step]] for cycle_step in range(SEGMENT_STEPS)], axis=0)
    fft_length = 2 * TOKENS
    filter_spec = jnp.fft.rfft(filter_taps, n=fft_length, axis=0)
    block_width = math.gcd(CHANNELS, 512)
    block_count = CHANNELS // block_width
    group_width = block_width // GROUP_CH

    def one_block(block_index):
        columns = lax.dynamic_slice_in_dim(mixed, block_index * block_width, block_width, 1)
        spectrum = jnp.fft.rfft(columns, n=fft_length, axis=0)
        group_spec = lax.dynamic_slice_in_dim(filter_spec, block_index * group_width, group_width, 1)
        group_spec = jnp.repeat(group_spec, GROUP_CH, axis=1)
        return jnp.fft.irfft(spectrum * group_spec, n=fft_length, axis=0)[:TOKENS]

    conv_blocks = lax.map(one_block, jnp.arange(block_count, dtype=jnp.int32))
    conv_out = jnp.transpose(conv_blocks, (1, 0, 2)).reshape(TOKENS, CHANNELS)
    return queries * (conv_out + skip_gain[None, :] * mixed)
```

```python
import jax
import jax.numpy as jnp
from jax import lax
from jax.sharding import PartitionSpec as P

HIGHEST = lax.Precision.HIGHEST
CHUNKS = 4


def from_root(block, axis, owner):
    block = jnp.where(lax.axis_index(axis) == owner, block, jnp.zeros_like(block))
    return lax.psum(block, axis)


def tables(length):
    freq_rows = lax.broadcasted_iota(jnp.int32, (length, length), 0)
    place_cols = lax.broadcasted_iota(jnp.int32, (length, length), 1)
    angle = jnp.pi * (freq_rows * place_cols % (2 * length)).astype(jnp.float32) / length
    parity = 1.0 - 2.0 * (place_cols % 2).astype(jnp.float32)
    fwd_real = jnp.cos(angle)
    fwd_imag = jnp.where(freq_rows == 0, parity, -jnp.sin(angle))
    out_place = freq_rows + length
    back_angle = jnp.pi * (place_cols * out_place % (2 * length)).astype(jnp.float32) / length
    out_parity = 1.0 - 2.0 * (out_place % 2).astype(jnp.float32)
    inv_real = jnp.where(place_cols == 0, 1.0, 2.0 * jnp.cos(back_angle)) / (2 * length)
    inv_imag = jnp.where(place_cols == 0, out_parity, -2.0 * jnp.sin(back_angle)) / (2 * length)
    return (fwd_real, fwd_imag, inv_real, inv_imag)


def transform(block, fwd_real, fwd_imag):
    return jnp.stack(
        [jnp.dot(fwd_real, block, precision=HIGHEST), jnp.dot(fwd_imag, block, precision=HIGHEST)]
    )


def inverse(total, inv_real, inv_imag):
    return jnp.dot(inv_real, total[0], precision=HIGHEST) + jnp.dot(
        inv_imag, total[1], precision=HIGHEST
    )


def apply_filter(spectrum, filt):
    length = spectrum.shape[1]
    chan_width = spectrum.shape[2]
    group_dev = filt.shape[2]
    a_real = spectrum[0].reshape(length, group_dev, chan_width // group_dev)
    a_imag = spectrum[1].reshape(length, group_dev, chan_width // group_dev)
    e_real = filt[0][:, :, None]
    e_imag = filt[1][:, :, None]
    first_row = lax.broadcasted_iota(jnp.int32, (length, 1, 1), 0) == 0
    prod_real = jnp.where(first_row, a_real * e_real, a_real * e_real - a_imag * e_imag)
    prod_imag = jnp.where(first_row, a_imag * e_imag, a_real * e_imag + a_imag * e_real)
    return jnp.stack([prod_real.reshape(length, chan_width), prod_imag.reshape(length, chan_width)])


def filtered_sum(specs, filters):
    total = apply_filter(specs[0], filters[0])
    for spec, filt in zip(specs[1:], filters[1:]):
        total = total + apply_filter(spec, filt)
    return total


def body(queries, key_in, values_in, skip_gain, filter_tap_bank, lag_slot):
    length, chan_width = key_in.shape
    slots_dev = filter_tap_bank.shape[0]
    cycle_steps = lag_slot.shape[0]
    group_dev = filter_tap_bank.shape[2] // lax.axis_size("sub")
    n_ctx = lax.axis_size("ctx")
    sub_index = lax.axis_index("sub")
    mixed_input = key_in * values_in
    fwd_real, fwd_imag, inv_real, inv_imag = tables(length)
    pieces = []
    for cycle_step in range(cycle_steps):
        slot_index = lag_slot[cycle_step]
        held_piece = lax.dynamic_index_in_dim(
            filter_tap_bank, slot_index % slots_dev, 0, keepdims=False
        )
        pieces.append(from_root(held_piece, ("ctx", "sub"), slot_index // slots_dev))
    filter_taps = jnp.concatenate(
        [lax.dynamic_slice_in_dim(piece, sub_index * group_dev, group_dev, 1) for piece in pieces],
        axis=1,
    )
    filter_spec = transform(filter_taps, fwd_real, fwd_imag)
    row_sign = (
        1.0 - 2.0 * (lax.broadcasted_iota(jnp.int32, (length, 1), 0) % 2).astype(jnp.float32)
    )[None]
    segment_spec = [
        filter_spec[:, :, cycle_step * group_dev : (cycle_step + 1) * group_dev]
        for cycle_step in range(cycle_steps)
    ]
    effective = [row_sign * segment_spec[0]]
    for cycle_step in range(1, cycle_steps):
        effective.append(segment_spec[cycle_step - 1] + row_sign * segment_spec[cycle_step])
    effective.append(segment_spec[cycle_steps - 1])

    last_raw = max(n_ctx - 2, 0)
    raw_rounds = min(cycle_steps, last_raw)
    part_terms = min(cycle_steps, raw_rounds + 1)
    chunks = CHUNKS if chan_width % (CHUNKS * 128) == 0 and group_dev % CHUNKS == 0 else 1
    chunk_w = chan_width // chunks
    chunk_g = group_dev // chunks
    outs = []
    for chunk in range(chunks):
        cols = slice(chunk * chunk_w, (chunk + 1) * chunk_w)
        groups = slice(chunk * chunk_g, (chunk + 1) * chunk_g)
        filters = [e[:, :, groups] for e in effective]
        moving = mixed_input[:, cols]
        blocks = [moving]
        for step in range(1, raw_rounds + 1):
            route = [(k, k + 1) for k in range(step - 1, last_raw)]
            moving = lax.ppermute(moving, "ctx", route)
            blocks.append(moving)
        specs = [transform(b, fwd_real, fwd_imag) for b in blocks]
        conv_out = inverse(filtered_sum(specs, filters), inv_real, inv_imag)
        if n_ctx >= 2:
            partial = inverse(
                filtered_sum(specs[:part_terms], filters[1 : part_terms + 1]), inv_real, inv_imag
            )
            conv_out = conv_out + lax.ppermute(partial, "ctx", [(last_raw, last_raw + 1)])
        gain = skip_gain[None, cols]
        outs.append(queries[:, cols] * (conv_out + gain * mixed_input[:, cols]))
    return jnp.concatenate(outs, axis=1) if chunks > 1 else outs[0]


def solution(mesh):
    in_specs = (
        P(("groups", "ctx"), ("chan", "sub")),
        P(("groups", "ctx"), ("chan", "sub")),
        P(("groups", "ctx"), ("chan", "sub")),
        P(("chan", "sub")),
        P(("ctx", "sub"), None, "chan"),
        P(),
    )
    out_specs = P(("groups", "ctx"), ("chan", "sub"))
    return jax.shard_map(body, mesh=mesh, in_specs=in_specs, out_specs=out_specs, check_vma=False)
```

```python
import jax
import jax.numpy as jnp
from jax import lax
from jax.sharding import PartitionSpec as P

HIGHEST = lax.Precision.HIGHEST
CHUNKS = 4


def from_root(block, axis, owner):
    block = jnp.where(lax.axis_index(axis) == owner, block, jnp.zeros_like(block))
    return lax.psum(block, axis)


def tables(length):
    freq_rows = lax.broadcasted_iota(jnp.int32, (length, length), 0)
    place_cols = lax.broadcasted_iota(jnp.int32, (length, length), 1)
    angle = jnp.pi * (freq_rows * place_cols % (2 * length)).astype(jnp.float32) / length
    parity = 1.0 - 2.0 * (place_cols % 2).astype(jnp.float32)
    fwd_real = jnp.cos(angle)
    fwd_imag = jnp.where(freq_rows == 0, parity, -jnp.sin(angle))
    out_place = freq_rows + length
    back_angle = jnp.pi * (place_cols * out_place % (2 * length)).astype(jnp.float32) / length
    out_parity = 1.0 - 2.0 * (out_place % 2).astype(jnp.float32)
    inv_real = jnp.where(place_cols == 0, 1.0, 2.0 * jnp.cos(back_angle)) / (2 * length)
    inv_imag = jnp.where(place_cols == 0, out_parity, -2.0 * jnp.sin(back_angle)) / (2 * length)
    return (fwd_real, fwd_imag, inv_real, inv_imag)


def transform(block, fwd_real, fwd_imag):
    return jnp.stack(
        [jnp.dot(fwd_real, block, precision=HIGHEST), jnp.dot(fwd_imag, block, precision=HIGHEST)]
    )


def inverse(total, inv_real, inv_imag):
    return jnp.dot(inv_real, total[0], precision=HIGHEST) + jnp.dot(
        inv_imag, total[1], precision=HIGHEST
    )


def apply_filter(spectrum, filt):
    length = spectrum.shape[1]
    chan_width = spectrum.shape[2]
    group_dev = filt.shape[2]
    a_real = spectrum[0].reshape(length, chan_width // group_dev, group_dev)
    a_imag = spectrum[1].reshape(length, chan_width // group_dev, group_dev)
    e_real = filt[0][:, None, :]
    e_imag = filt[1][:, None, :]
    first_row = lax.broadcasted_iota(jnp.int32, (length, 1, 1), 0) == 0
    prod_real = jnp.where(first_row, a_real * e_real, a_real * e_real - a_imag * e_imag)
    prod_imag = jnp.where(first_row, a_imag * e_imag, a_real * e_imag + a_imag * e_real)
    return jnp.stack([prod_real.reshape(length, chan_width), prod_imag.reshape(length, chan_width)])


def filtered_sum(specs, filters):
    total = apply_filter(specs[0], filters[0])
    for spec, filt in zip(specs[1:], filters[1:]):
        total = total + apply_filter(spec, filt)
    return total


def body(queries, key_in, values_in, skip_gain, filter_tap_bank, lag_slot):
    length, chan_width = key_in.shape
    slots_dev = filter_tap_bank.shape[0]
    cycle_steps = lag_slot.shape[0]
    group_dev = filter_tap_bank.shape[2] // lax.axis_size("sub")
    n_ctx = lax.axis_size("ctx")
    sub_index = lax.axis_index("sub")
    mixed_input = key_in * values_in
    fwd_real, fwd_imag, inv_real, inv_imag = lax.optimization_barrier(tables(length))
    members = chan_width // group_dev
    member_major = (
        mixed_input.reshape(length, group_dev, members).transpose(0, 2, 1).reshape(length, chan_width)
    )
    pieces = []
    for cycle_step in range(cycle_steps):
        slot_index = lag_slot[cycle_step]
        held_piece = lax.dynamic_index_in_dim(
            filter_tap_bank, slot_index % slots_dev, 0, keepdims=False
        )
        owner = slot_index // slots_dev
        chip_piece = from_root(held_piece, "sub", owner % lax.axis_size("sub"))
        half = lax.dynamic_slice_in_dim(chip_piece, sub_index * group_dev, group_dev, 1)
        pieces.append(from_root(half, "ctx", owner // lax.axis_size("sub")))
    filter_taps = jnp.concatenate(pieces, axis=1)
    filter_spec = transform(filter_taps, fwd_real, fwd_imag)
    row_sign = (
        1.0 - 2.0 * (lax.broadcasted_iota(jnp.int32, (length, 1), 0) % 2).astype(jnp.float32)
    )[None]
    segment_spec = [
        filter_spec[:, :, cycle_step * group_dev : (cycle_step + 1) * group_dev]
        for cycle_step in range(cycle_steps)
    ]
    effective = [row_sign * segment_spec[0]]
    for cycle_step in range(1, cycle_steps):
        effective.append(segment_spec[cycle_step - 1] + row_sign * segment_spec[cycle_step])
    effective.append(segment_spec[cycle_steps - 1])

    last_raw = max(n_ctx - 2, 0)
    raw_rounds = min(cycle_steps, last_raw)
    part_terms = min(cycle_steps, raw_rounds + 1)
    chunks = CHUNKS if members % CHUNKS == 0 else 1
    chunk_w = chan_width // chunks
    outs = []
    for chunk in range(chunks):
        cols = slice(chunk * chunk_w, (chunk + 1) * chunk_w)
        filters = effective
        moving = member_major[:, cols]
        blocks = [moving]
        for step in range(1, raw_rounds + 1):
            route = [(k, k + 1) for k in range(step - 1, last_raw)]
            moving = lax.ppermute(moving, "ctx", route)
            blocks.append(moving)
        specs = [transform(b, fwd_real, fwd_imag) for b in blocks]
        conv_out = inverse(filtered_sum(specs, filters), inv_real, inv_imag)
        if n_ctx >= 2:
            partial = inverse(
                filtered_sum(specs[:part_terms], filters[1 : part_terms + 1]), inv_real, inv_imag
            )
            conv_out = conv_out + lax.ppermute(partial, "ctx", [(last_raw, last_raw + 1)])
        outs.append(conv_out)
    conv_all = jnp.concatenate(outs, axis=1) if chunks > 1 else outs[0]
    conv_all = conv_all.reshape(length, members, group_dev).transpose(0, 2, 1).reshape(length, chan_width)
    return queries * (conv_all + skip_gain[None, :] * mixed_input)


def solution(mesh):
    in_specs = (
        P(("groups", "ctx"), ("chan", "sub")),
        P(("groups", "ctx"), ("chan", "sub")),
        P(("groups", "ctx"), ("chan", "sub")),
        P(("chan", "sub")),
        P(("ctx", "sub"), None, "chan"),
        P(),
    )
    out_specs = P(("groups", "ctx"), ("chan", "sub"))
    return jax.shard_map(body, mesh=mesh, in_specs=in_specs, out_specs=out_specs, check_vma=False)
```

```python
import jax
import jax.numpy as jnp
from jax import lax
from jax.sharding import PartitionSpec as P

HIGHEST = lax.Precision.HIGHEST
CHUNKS = 4


def from_root(block, axis, owner):
    block = jnp.where(lax.axis_index(axis) == owner, block, jnp.zeros_like(block))
    return lax.psum(block, axis)


def tables(length):
    freq_rows = lax.broadcasted_iota(jnp.int32, (length, length), 0)
    place_cols = lax.broadcasted_iota(jnp.int32, (length, length), 1)
    angle = jnp.pi * (freq_rows * place_cols % (2 * length)).astype(jnp.float32) / length
    parity = 1.0 - 2.0 * (place_cols % 2).astype(jnp.float32)
    fwd_real = jnp.cos(angle)
    fwd_imag = jnp.where(freq_rows == 0, parity, -jnp.sin(angle))
    out_place = freq_rows + length
    back_angle = jnp.pi * (place_cols * out_place % (2 * length)).astype(jnp.float32) / length
    out_parity = 1.0 - 2.0 * (out_place % 2).astype(jnp.float32)
    inv_real = jnp.where(place_cols == 0, 1.0, 2.0 * jnp.cos(back_angle)) / (2 * length)
    inv_imag = jnp.where(place_cols == 0, out_parity, -2.0 * jnp.sin(back_angle)) / (2 * length)
    return (fwd_real, fwd_imag, inv_real, inv_imag)


def transform(block, fwd_real, fwd_imag):
    return jnp.stack(
        [jnp.dot(fwd_real, block, precision=HIGHEST), jnp.dot(fwd_imag, block, precision=HIGHEST)]
    )


def inverse(total, inv_real, inv_imag):
    return jnp.dot(inv_real, total[0], precision=HIGHEST) + jnp.dot(
        inv_imag, total[1], precision=HIGHEST
    )


def apply_filter(spectrum, filt):
    length = spectrum.shape[1]
    chan_width = spectrum.shape[2]
    group_dev = filt.shape[2]
    a_real = spectrum[0].reshape(length, chan_width // group_dev, group_dev)
    a_imag = spectrum[1].reshape(length, chan_width // group_dev, group_dev)
    e_real = filt[0][:, None, :]
    e_imag = filt[1][:, None, :]
    first_row = lax.broadcasted_iota(jnp.int32, (length, 1, 1), 0) == 0
    prod_real = jnp.where(first_row, a_real * e_real, a_real * e_real - a_imag * e_imag)
    prod_imag = jnp.where(first_row, a_imag * e_imag, a_real * e_imag + a_imag * e_real)
    return jnp.stack([prod_real.reshape(length, chan_width), prod_imag.reshape(length, chan_width)])


def filtered_sum(specs, filters):
    total = apply_filter(specs[0], filters[0])
    for spec, filt in zip(specs[1:], filters[1:]):
        total = total + apply_filter(spec, filt)
    return total


def body(queries, key_in, values_in, skip_gain, filter_tap_bank, lag_slot):
    length, chan_width = key_in.shape
    slots_dev = filter_tap_bank.shape[0]
    cycle_steps = lag_slot.shape[0]
    group_dev = filter_tap_bank.shape[2] // lax.axis_size("sub")
    n_ctx = lax.axis_size("ctx")
    sub_index = lax.axis_index("sub")
    mixed_input = key_in * values_in
    fwd_real, fwd_imag, inv_real, inv_imag = lax.optimization_barrier(tables(length))
    members = chan_width // group_dev
    member_major = (
        mixed_input.reshape(length, group_dev, members).transpose(0, 2, 1).reshape(length, chan_width)
    )
    n_sub = lax.axis_size("sub")
    received = []
    for offset in range(n_sub):
        wanted = lax.dynamic_slice_in_dim(
            filter_tap_bank, ((sub_index + offset) % n_sub) * group_dev, group_dev, 2
        )
        if offset:
            wanted = lax.ppermute(
                wanted, "sub", [(i, (i + offset) % n_sub) for i in range(n_sub)]
            )
        received.append(wanted)
    received = jnp.stack(received)
    pieces = []
    for cycle_step in range(cycle_steps):
        slot_index = lag_slot[cycle_step]
        owner = slot_index // slots_dev
        source = (sub_index - owner % n_sub) % n_sub
        held_piece = received[source, slot_index % slots_dev]
        pieces.append(from_root(held_piece, "ctx", owner // n_sub))
    filter_taps = jnp.concatenate(pieces, axis=1)
    filter_spec = transform(filter_taps, fwd_real, fwd_imag)
    row_sign = (
        1.0 - 2.0 * (lax.broadcasted_iota(jnp.int32, (length, 1), 0) % 2).astype(jnp.float32)
    )[None]
    segment_spec = [
        filter_spec[:, :, cycle_step * group_dev : (cycle_step + 1) * group_dev]
        for cycle_step in range(cycle_steps)
    ]
    effective = [row_sign * segment_spec[0]]
    for cycle_step in range(1, cycle_steps):
        effective.append(segment_spec[cycle_step - 1] + row_sign * segment_spec[cycle_step])
    effective.append(segment_spec[cycle_steps - 1])

    last_raw = max(n_ctx - 2, 0)
    raw_rounds = min(cycle_steps, last_raw)
    part_terms = min(cycle_steps, raw_rounds + 1)
    chunks = CHUNKS if members % CHUNKS == 0 else 1
    chunk_w = chan_width // chunks
    outs = []
    for chunk in range(chunks):
        cols = slice(chunk * chunk_w, (chunk + 1) * chunk_w)
        filters = effective
        moving = member_major[:, cols]
        blocks = [moving]
        for step in range(1, raw_rounds + 1):
            route = [(k, k + 1) for k in range(step - 1, last_raw)]
            moving = lax.ppermute(moving, "ctx", route)
            blocks.append(moving)
        specs = [transform(b, fwd_real, fwd_imag) for b in blocks]
        conv_out = inverse(filtered_sum(specs, filters), inv_real, inv_imag)
        if n_ctx >= 2:
            partial = inverse(
                filtered_sum(specs[:part_terms], filters[1 : part_terms + 1]), inv_real, inv_imag
            )
            conv_out = conv_out + lax.ppermute(partial, "ctx", [(last_raw, last_raw + 1)])
        outs.append(conv_out)
    conv_all = jnp.concatenate(outs, axis=1) if chunks > 1 else outs[0]
    conv_all = conv_all.reshape(length, members, group_dev).transpose(0, 2, 1).reshape(length, chan_width)
    return queries * (conv_all + skip_gain[None, :] * mixed_input)


def solution(mesh):
    in_specs = (
        P(("groups", "ctx"), ("chan", "sub")),
        P(("groups", "ctx"), ("chan", "sub")),
        P(("groups", "ctx"), ("chan", "sub")),
        P(("chan", "sub")),
        P(("ctx", "sub"), None, "chan"),
        P(),
    )
    out_specs = P(("groups", "ctx"), ("chan", "sub"))
    return jax.shard_map(body, mesh=mesh, in_specs=in_specs, out_specs=out_specs, check_vma=False)
```

```python
import jax
import jax.numpy as jnp
from jax import lax
from jax.sharding import PartitionSpec as P

HIGHEST = lax.Precision.HIGHEST
DATA_PRECISION = lax.Precision.HIGH
CHUNKS = 4


def from_root(block, axis, owner):
    block = jnp.where(lax.axis_index(axis) == owner, block, jnp.zeros_like(block))
    return lax.psum(block, axis)


def tables(length):
    freq_rows = lax.broadcasted_iota(jnp.int32, (length, length), 0)
    place_cols = lax.broadcasted_iota(jnp.int32, (length, length), 1)
    angle = jnp.pi * (freq_rows * place_cols % (2 * length)).astype(jnp.float32) / length
    parity = 1.0 - 2.0 * (place_cols % 2).astype(jnp.float32)
    fwd_real = jnp.cos(angle)
    fwd_imag = jnp.where(freq_rows == 0, parity, -jnp.sin(angle))
    out_place = freq_rows + length
    back_angle = jnp.pi * (place_cols * out_place % (2 * length)).astype(jnp.float32) / length
    out_parity = 1.0 - 2.0 * (out_place % 2).astype(jnp.float32)
    inv_real = jnp.where(place_cols == 0, 1.0, 2.0 * jnp.cos(back_angle)) / (2 * length)
    inv_imag = jnp.where(place_cols == 0, out_parity, -2.0 * jnp.sin(back_angle)) / (2 * length)
    return (fwd_real, fwd_imag, inv_real, inv_imag)


def transform(block, fwd_real, fwd_imag, precision=DATA_PRECISION):
    return jnp.stack(
        [jnp.dot(fwd_real, block, precision=precision), jnp.dot(fwd_imag, block, precision=precision)]
    )


def inverse(total, inv_real, inv_imag):
    return jnp.dot(inv_real, total[0], precision=DATA_PRECISION) + jnp.dot(
        inv_imag, total[1], precision=DATA_PRECISION
    )


def apply_filter(spectrum, filt):
    length = spectrum.shape[1]
    chan_width = spectrum.shape[2]
    group_dev = filt.shape[2]
    a_real = spectrum[0].reshape(length, chan_width // group_dev, group_dev)
    a_imag = spectrum[1].reshape(length, chan_width // group_dev, group_dev)
    e_real = filt[0][:, None, :]
    e_imag = filt[1][:, None, :]
    first_row = lax.broadcasted_iota(jnp.int32, (length, 1, 1), 0) == 0
    prod_real = jnp.where(first_row, a_real * e_real, a_real * e_real - a_imag * e_imag)
    prod_imag = jnp.where(first_row, a_imag * e_imag, a_real * e_imag + a_imag * e_real)
    return jnp.stack([prod_real.reshape(length, chan_width), prod_imag.reshape(length, chan_width)])


def filtered_sum(specs, filters):
    total = apply_filter(specs[0], filters[0])
    for spec, filt in zip(specs[1:], filters[1:]):
        total = total + apply_filter(spec, filt)
    return total


def body(queries, key_in, values_in, skip_gain, filter_tap_bank, lag_slot):
    length, chan_width = key_in.shape
    slots_dev = filter_tap_bank.shape[0]
    cycle_steps = lag_slot.shape[0]
    group_dev = filter_tap_bank.shape[2] // lax.axis_size("sub")
    n_ctx = lax.axis_size("ctx")
    sub_index = lax.axis_index("sub")
    mixed_input = key_in * values_in
    fwd_real, fwd_imag, inv_real, inv_imag = lax.optimization_barrier(tables(length))
    members = chan_width // group_dev
    member_major = (
        mixed_input.reshape(length, group_dev, members).transpose(0, 2, 1).reshape(length, chan_width)
    )
    n_sub = lax.axis_size("sub")
    received = []
    for offset in range(n_sub):
        wanted = lax.dynamic_slice_in_dim(
            filter_tap_bank, ((sub_index + offset) % n_sub) * group_dev, group_dev, 2
        )
        if offset:
            wanted = lax.ppermute(
                wanted, "sub", [(i, (i + offset) % n_sub) for i in range(n_sub)]
            )
        received.append(wanted)
    received = jnp.stack(received)
    member_major, received = lax.optimization_barrier((member_major, received))
    pieces = []
    for cycle_step in range(cycle_steps):
        slot_index = lag_slot[cycle_step]
        owner = slot_index // slots_dev
        source = (sub_index - owner % n_sub) % n_sub
        held_piece = received[source, slot_index % slots_dev]
        pieces.append(from_root(held_piece, "ctx", owner // n_sub))
    filter_taps = jnp.concatenate(pieces, axis=1)
    filter_spec = transform(filter_taps, fwd_real, fwd_imag, HIGHEST)
    row_sign = (
        1.0 - 2.0 * (lax.broadcasted_iota(jnp.int32, (length, 1), 0) % 2).astype(jnp.float32)
    )[None]
    segment_spec = [
        filter_spec[:, :, cycle_step * group_dev : (cycle_step + 1) * group_dev]
        for cycle_step in range(cycle_steps)
    ]
    effective = [row_sign * segment_spec[0]]
    for cycle_step in range(1, cycle_steps):
        effective.append(segment_spec[cycle_step - 1] + row_sign * segment_spec[cycle_step])
    effective.append(segment_spec[cycle_steps - 1])

    last_raw = max(n_ctx - 2, 0)
    raw_rounds = min(cycle_steps, last_raw)
    part_terms = min(cycle_steps, raw_rounds + 1)
    chunks = CHUNKS if members % CHUNKS == 0 else 1
    chunk_w = chan_width // chunks
    outs = []
    previous = None
    sent = None
    pending = None
    for chunk in range(chunks):
        cols = slice(chunk * chunk_w, (chunk + 1) * chunk_w)
        filters = effective
        moving = member_major[:, cols]
        if previous is not None:
            moving, _ = lax.optimization_barrier((moving, previous))
        blocks = [moving]
        for step in range(1, raw_rounds + 1):
            route = [(k, k + 1) for k in range(step - 1, last_raw)]
            if step == raw_rounds and step > 1 and pending is not None:
                moving, _ = lax.optimization_barrier((moving, pending))
            moving = lax.ppermute(moving, "ctx", route)
            blocks.append(moving)
        if raw_rounds:
            previous = blocks[1]
        specs = [transform(b, fwd_real, fwd_imag) for b in blocks]
        conv_out = inverse(filtered_sum(specs, filters), inv_real, inv_imag)
        if n_ctx >= 2:
            part_specs = specs[:part_terms]
            if sent is not None:
                part_specs, _ = lax.optimization_barrier((part_specs, sent))
            partial = inverse(
                filtered_sum(part_specs, filters[1 : part_terms + 1]), inv_real, inv_imag
            )
            pending = partial
            sent = lax.ppermute(partial, "ctx", [(last_raw, last_raw + 1)])
            conv_out = conv_out + sent
        outs.append(conv_out)
    conv_all = jnp.concatenate(outs, axis=1) if chunks > 1 else outs[0]
    conv_all = conv_all.reshape(length, members, group_dev).transpose(0, 2, 1).reshape(length, chan_width)
    return queries * (conv_all + skip_gain[None, :] * mixed_input)


def solution(mesh):
    in_specs = (
        P(("groups", "ctx"), ("chan", "sub")),
        P(("groups", "ctx"), ("chan", "sub")),
        P(("groups", "ctx"), ("chan", "sub")),
        P(("chan", "sub")),
        P(("ctx", "sub"), None, "chan"),
        P(),
    )
    out_specs = P(("groups", "ctx"), ("chan", "sub"))
    return jax.shard_map(body, mesh=mesh, in_specs=in_specs, out_specs=out_specs, check_vma=False)
```

```python
import jax
import jax.numpy as jnp
from jax import lax
from jax.sharding import PartitionSpec as P

HIGHEST = lax.Precision.HIGHEST
DATA_PRECISION = lax.Precision.HIGH
CHUNKS = 4


def from_root(block, axis, owner):
    block = jnp.where(lax.axis_index(axis) == owner, block, jnp.zeros_like(block))
    return lax.psum(block, axis)


def tables(length):
    freq_rows = lax.broadcasted_iota(jnp.int32, (length, length), 0)
    place_cols = lax.broadcasted_iota(jnp.int32, (length, length), 1)
    angle = jnp.pi * (freq_rows * place_cols % (2 * length)).astype(jnp.float32) / length
    parity = 1.0 - 2.0 * (place_cols % 2).astype(jnp.float32)
    fwd_real = jnp.cos(angle)
    fwd_imag = jnp.where(freq_rows == 0, parity, -jnp.sin(angle))
    out_place = freq_rows + length
    back_angle = jnp.pi * (place_cols * out_place % (2 * length)).astype(jnp.float32) / length
    out_parity = 1.0 - 2.0 * (out_place % 2).astype(jnp.float32)
    inv_real = jnp.where(place_cols == 0, 1.0, 2.0 * jnp.cos(back_angle)) / (2 * length)
    inv_imag = jnp.where(place_cols == 0, out_parity, -2.0 * jnp.sin(back_angle)) / (2 * length)
    return (fwd_real, fwd_imag, inv_real, inv_imag)


def transform(block, fwd_real, fwd_imag, precision=DATA_PRECISION):
    return jnp.stack(
        [jnp.dot(fwd_real, block, precision=precision), jnp.dot(fwd_imag, block, precision=precision)]
    )


def inverse(total, inv_real, inv_imag):
    return jnp.dot(inv_real, total[0], precision=DATA_PRECISION) + jnp.dot(
        inv_imag, total[1], precision=DATA_PRECISION
    )


def apply_filter(spectrum, filt):
    length = spectrum.shape[1]
    chan_width = spectrum.shape[2]
    group_dev = filt.shape[2]
    a_real = spectrum[0].reshape(length, chan_width // group_dev, group_dev)
    a_imag = spectrum[1].reshape(length, chan_width // group_dev, group_dev)
    e_real = filt[0][:, None, :]
    e_imag = filt[1][:, None, :]
    first_row = lax.broadcasted_iota(jnp.int32, (length, 1, 1), 0) == 0
    prod_real = jnp.where(first_row, a_real * e_real, a_real * e_real - a_imag * e_imag)
    prod_imag = jnp.where(first_row, a_imag * e_imag, a_real * e_imag + a_imag * e_real)
    return jnp.stack([prod_real.reshape(length, chan_width), prod_imag.reshape(length, chan_width)])


def filtered_sum(specs, filters):
    total = apply_filter(specs[0], filters[0])
    for spec, filt in zip(specs[1:], filters[1:]):
        total = total + apply_filter(spec, filt)
    return total


def body(queries, key_in, values_in, skip_gain, filter_tap_bank, lag_slot):
    length, chan_width = key_in.shape
    slots_dev = filter_tap_bank.shape[0]
    cycle_steps = lag_slot.shape[0]
    group_dev = filter_tap_bank.shape[2] // lax.axis_size("sub")
    n_ctx = lax.axis_size("ctx")
    sub_index = lax.axis_index("sub")
    mixed_input = key_in * values_in
    fwd_real, fwd_imag, inv_real, inv_imag = lax.optimization_barrier(tables(length))
    members = chan_width // group_dev
    member_major = (
        mixed_input.reshape(length, group_dev, members).transpose(0, 2, 1).reshape(length, chan_width)
    )
    n_sub = lax.axis_size("sub")
    received = []
    for offset in range(n_sub):
        wanted = lax.dynamic_slice_in_dim(
            filter_tap_bank, ((sub_index + offset) % n_sub) * group_dev, group_dev, 2
        )
        if offset:
            wanted = lax.ppermute(
                wanted, "sub", [(i, (i + offset) % n_sub) for i in range(n_sub)]
            )
        received.append(wanted)
    received = jnp.stack(received)
    pieces = []
    for cycle_step in range(cycle_steps):
        slot_index = lag_slot[cycle_step]
        owner = slot_index // slots_dev
        source = (sub_index - owner % n_sub) % n_sub
        held_piece = received[source, slot_index % slots_dev]
        pieces.append(from_root(held_piece, "ctx", owner // n_sub))
    filter_taps = jnp.concatenate(pieces, axis=1)
    row_sign = (
        1.0 - 2.0 * (lax.broadcasted_iota(jnp.int32, (length, 1), 0) % 2).astype(jnp.float32)
    )[None]

    last_raw = max(n_ctx - 2, 0)
    raw_rounds = min(cycle_steps, last_raw)
    part_terms = min(cycle_steps, raw_rounds + 1)
    chunks = CHUNKS if members % CHUNKS == 0 else 1
    chunk_w = chan_width // chunks
    outs = []
    arrived = None
    sent = None
    partials = []
    effective = None
    for chunk in range(chunks):
        cols = slice(chunk * chunk_w, (chunk + 1) * chunk_w)
        own = member_major[:, cols]
        if arrived is not None:
            own, _ = lax.optimization_barrier((own, arrived))
        if chunk >= 2:
            own, _ = lax.optimization_barrier((own, partials[chunk - 2]))
        blocks = [own]
        for distance in range(1, raw_rounds + 1):
            route = [(k - distance, k) for k in range(distance, last_raw + 1)]
            blocks.append(lax.ppermute(own, "ctx", route))
        arrived = blocks[1:] if raw_rounds else None
        if effective is None:
            if arrived is not None:
                filter_taps, _ = lax.optimization_barrier((filter_taps, arrived))
            filter_spec = transform(filter_taps, fwd_real, fwd_imag, HIGHEST)
            segment_spec = [
                filter_spec[:, :, step * group_dev : (step + 1) * group_dev]
                for step in range(cycle_steps)
            ]
            effective = [row_sign * segment_spec[0]]
            for step in range(1, cycle_steps):
                effective.append(segment_spec[step - 1] + row_sign * segment_spec[step])
            effective.append(segment_spec[cycle_steps - 1])
        filters = effective
        specs = [transform(b, fwd_real, fwd_imag) for b in blocks]
        conv_out = inverse(filtered_sum(specs, filters), inv_real, inv_imag)
        if n_ctx >= 2:
            part_specs = specs[:part_terms]
            if sent is not None:
                part_specs, _ = lax.optimization_barrier((part_specs, sent))
            partial = inverse(
                filtered_sum(part_specs, filters[1 : part_terms + 1]), inv_real, inv_imag
            )
            partials.append(partial)
            sent = lax.ppermute(partial, "ctx", [(last_raw, last_raw + 1)])
            conv_out = conv_out + sent
        outs.append(conv_out)
    conv_all = jnp.concatenate(outs, axis=1) if chunks > 1 else outs[0]
    conv_all = conv_all.reshape(length, members, group_dev).transpose(0, 2, 1).reshape(length, chan_width)
    return queries * (conv_all + skip_gain[None, :] * mixed_input)


def solution(mesh):
    in_specs = (
        P(("groups", "ctx"), ("chan", "sub")),
        P(("groups", "ctx"), ("chan", "sub")),
        P(("groups", "ctx"), ("chan", "sub")),
        P(("chan", "sub")),
        P(("ctx", "sub"), None, "chan"),
        P(),
    )
    out_specs = P(("groups", "ctx"), ("chan", "sub"))
    return jax.shard_map(body, mesh=mesh, in_specs=in_specs, out_specs=out_specs, check_vma=False)
```

```python
import jax
import jax.numpy as jnp
from jax import lax
from jax.sharding import PartitionSpec as P

HIGHEST = lax.Precision.HIGHEST
DATA_PRECISION = lax.Precision.HIGH
CHUNKS = 4


def from_root(block, axis, owner):
    block = jnp.where(lax.axis_index(axis) == owner, block, jnp.zeros_like(block))
    return lax.psum(block, axis)


def tables(length):
    freq_rows = lax.broadcasted_iota(jnp.int32, (length, length), 0)
    place_cols = lax.broadcasted_iota(jnp.int32, (length, length), 1)
    angle = jnp.pi * (freq_rows * place_cols % (2 * length)).astype(jnp.float32) / length
    parity = 1.0 - 2.0 * (place_cols % 2).astype(jnp.float32)
    fwd_real = jnp.cos(angle)
    fwd_imag = jnp.where(freq_rows == 0, parity, -jnp.sin(angle))
    out_place = freq_rows + length
    back_angle = jnp.pi * (place_cols * out_place % (2 * length)).astype(jnp.float32) / length
    out_parity = 1.0 - 2.0 * (out_place % 2).astype(jnp.float32)
    inv_real = jnp.where(place_cols == 0, 1.0, 2.0 * jnp.cos(back_angle)) / (2 * length)
    inv_imag = jnp.where(place_cols == 0, out_parity, -2.0 * jnp.sin(back_angle)) / (2 * length)
    return (fwd_real, fwd_imag, inv_real, inv_imag)


def transform(block, fwd_real, fwd_imag, precision=DATA_PRECISION):
    return jnp.stack(
        [jnp.dot(fwd_real, block, precision=precision), jnp.dot(fwd_imag, block, precision=precision)]
    )


def inverse(total, inv_real, inv_imag):
    return jnp.dot(inv_real, total[0], precision=DATA_PRECISION) + jnp.dot(
        inv_imag, total[1], precision=DATA_PRECISION
    )


def apply_filter(spectrum, filt):
    length = spectrum.shape[1]
    chan_width = spectrum.shape[2]
    group_dev = filt.shape[2]
    a_real = spectrum[0].reshape(length, chan_width // group_dev, group_dev)
    a_imag = spectrum[1].reshape(length, chan_width // group_dev, group_dev)
    e_real = filt[0][:, None, :]
    e_imag = filt[1][:, None, :]
    first_row = lax.broadcasted_iota(jnp.int32, (length, 1, 1), 0) == 0
    prod_real = jnp.where(first_row, a_real * e_real, a_real * e_real - a_imag * e_imag)
    prod_imag = jnp.where(first_row, a_imag * e_imag, a_real * e_imag + a_imag * e_real)
    return jnp.stack([prod_real.reshape(length, chan_width), prod_imag.reshape(length, chan_width)])


def filtered_sum(specs, filters):
    total = apply_filter(specs[0], filters[0])
    for spec, filt in zip(specs[1:], filters[1:]):
        total = total + apply_filter(spec, filt)
    return total


def body(queries, key_in, values_in, skip_gain, filter_tap_bank, lag_slot):
    length, chan_width = key_in.shape
    slots_dev = filter_tap_bank.shape[0]
    cycle_steps = lag_slot.shape[0]
    group_dev = filter_tap_bank.shape[2] // lax.axis_size("sub")
    n_ctx = lax.axis_size("ctx")
    sub_index = lax.axis_index("sub")
    fwd_real, fwd_imag, inv_real, inv_imag = lax.optimization_barrier(tables(length))
    members = chan_width // group_dev
    n_sub = lax.axis_size("sub")
    received = []
    for offset in range(n_sub):
        wanted = lax.dynamic_slice_in_dim(
            filter_tap_bank, ((sub_index + offset) % n_sub) * group_dev, group_dev, 2
        )
        if offset:
            wanted = lax.ppermute(
                wanted, "sub", [(i, (i + offset) % n_sub) for i in range(n_sub)]
            )
        received.append(wanted)
    received = jnp.stack(received)
    pieces = []
    for cycle_step in range(cycle_steps):
        slot_index = lag_slot[cycle_step]
        owner = slot_index // slots_dev
        source = (sub_index - owner % n_sub) % n_sub
        held_piece = received[source, slot_index % slots_dev]
        owned = lax.axis_index("ctx") == owner // n_sub
        pieces.append(jnp.where(owned, held_piece, jnp.zeros_like(held_piece)))
    key_in, values_in, pieces = lax.optimization_barrier((key_in, values_in, pieces))
    filter_taps = jnp.concatenate(lax.psum(pieces, "ctx"), axis=1)
    mixed_input = key_in * values_in
    member_major = (
        mixed_input.reshape(length, group_dev, members).transpose(0, 2, 1).reshape(length, chan_width)
    )
    row_sign = (
        1.0 - 2.0 * (lax.broadcasted_iota(jnp.int32, (length, 1), 0) % 2).astype(jnp.float32)
    )[None]

    last_raw = max(n_ctx - 2, 0)
    raw_rounds = min(cycle_steps, last_raw)
    part_terms = min(cycle_steps, raw_rounds + 1)
    chunks = CHUNKS if members % CHUNKS == 0 else 1
    chunk_w = chan_width // chunks
    outs = []
    arrived = None
    sent = None
    partials = []
    effective = None
    for chunk in range(chunks):
        cols = slice(chunk * chunk_w, (chunk + 1) * chunk_w)
        own = member_major[:, cols]
        if arrived is not None:
            own, _ = lax.optimization_barrier((own, arrived))
        if chunk >= 2:
            own, _ = lax.optimization_barrier((own, partials[chunk - 2]))
        blocks = [own]
        for distance in range(1, raw_rounds + 1):
            route = [(k - distance, k) for k in range(distance, last_raw + 1)]
            blocks.append(lax.ppermute(own, "ctx", route))
        arrived = blocks[1:] if raw_rounds else None
        if effective is None:
            if arrived is not None:
                filter_taps, _ = lax.optimization_barrier((filter_taps, arrived))
            filter_spec = transform(filter_taps, fwd_real, fwd_imag, HIGHEST)
            segment_spec = [
                filter_spec[:, :, step * group_dev : (step + 1) * group_dev]
                for step in range(cycle_steps)
            ]
            effective = [row_sign * segment_spec[0]]
            for step in range(1, cycle_steps):
                effective.append(segment_spec[step - 1] + row_sign * segment_spec[step])
            effective.append(segment_spec[cycle_steps - 1])
        filters = effective
        specs = [transform(b, fwd_real, fwd_imag) for b in blocks]
        conv_out = inverse(filtered_sum(specs, filters), inv_real, inv_imag)
        if n_ctx >= 2:
            part_specs = specs[:part_terms]
            if sent is not None:
                part_specs, _ = lax.optimization_barrier((part_specs, sent))
            partial = inverse(
                filtered_sum(part_specs, filters[1 : part_terms + 1]), inv_real, inv_imag
            )
            partials.append(partial)
            sent = lax.ppermute(partial, "ctx", [(last_raw, last_raw + 1)])
            conv_out = conv_out + sent
        outs.append(conv_out)
    conv_all = jnp.concatenate(outs, axis=1) if chunks > 1 else outs[0]
    conv_all = conv_all.reshape(length, members, group_dev).transpose(0, 2, 1).reshape(length, chan_width)
    return queries * (conv_all + skip_gain[None, :] * mixed_input)


def solution(mesh):
    in_specs = (
        P(("groups", "ctx"), ("chan", "sub")),
        P(("groups", "ctx"), ("chan", "sub")),
        P(("groups", "ctx"), ("chan", "sub")),
        P(("chan", "sub")),
        P(("ctx", "sub"), None, "chan"),
        P(),
    )
    out_specs = P(("groups", "ctx"), ("chan", "sub"))
    return jax.shard_map(body, mesh=mesh, in_specs=in_specs, out_specs=out_specs, check_vma=False)
```

```python
import jax
import jax.numpy as jnp
from jax import lax
from jax.sharding import PartitionSpec as P

HIGHEST = lax.Precision.HIGHEST
DATA_PRECISION = lax.Precision.HIGH
CHUNKS = 4


def from_root(block, axis, owner):
    block = jnp.where(lax.axis_index(axis) == owner, block, jnp.zeros_like(block))
    return lax.psum(block, axis)


def tables(length):
    freq_rows = lax.broadcasted_iota(jnp.int32, (length, length), 0)
    place_cols = lax.broadcasted_iota(jnp.int32, (length, length), 1)
    angle = jnp.pi * (freq_rows * place_cols % (2 * length)).astype(jnp.float32) / length
    parity = 1.0 - 2.0 * (place_cols % 2).astype(jnp.float32)
    fwd_real = jnp.cos(angle)
    fwd_imag = jnp.where(freq_rows == 0, parity, -jnp.sin(angle))
    out_place = freq_rows + length
    back_angle = jnp.pi * (place_cols * out_place % (2 * length)).astype(jnp.float32) / length
    out_parity = 1.0 - 2.0 * (out_place % 2).astype(jnp.float32)
    inv_real = jnp.where(place_cols == 0, 1.0, 2.0 * jnp.cos(back_angle)) / (2 * length)
    inv_imag = jnp.where(place_cols == 0, out_parity, -2.0 * jnp.sin(back_angle)) / (2 * length)
    return (fwd_real, fwd_imag, inv_real, inv_imag)


def transform(block, fwd_real, fwd_imag, precision=DATA_PRECISION):
    return jnp.stack(
        [jnp.dot(fwd_real, block, precision=precision), jnp.dot(fwd_imag, block, precision=precision)]
    )


def inverse(total, inv_real, inv_imag):
    return jnp.dot(inv_real, total[0], precision=DATA_PRECISION) + jnp.dot(
        inv_imag, total[1], precision=DATA_PRECISION
    )


def apply_filter(spectrum, filt):
    length = spectrum.shape[1]
    chan_width = spectrum.shape[2]
    group_dev = filt.shape[2]
    a_real = spectrum[0].reshape(length, chan_width // group_dev, group_dev)
    a_imag = spectrum[1].reshape(length, chan_width // group_dev, group_dev)
    e_real = filt[0][:, None, :]
    e_imag = filt[1][:, None, :]
    first_row = lax.broadcasted_iota(jnp.int32, (length, 1, 1), 0) == 0
    prod_real = jnp.where(first_row, a_real * e_real, a_real * e_real - a_imag * e_imag)
    prod_imag = jnp.where(first_row, a_imag * e_imag, a_real * e_imag + a_imag * e_real)
    return jnp.stack([prod_real.reshape(length, chan_width), prod_imag.reshape(length, chan_width)])


def filtered_sum(specs, filters):
    total = apply_filter(specs[0], filters[0])
    for spec, filt in zip(specs[1:], filters[1:]):
        total = total + apply_filter(spec, filt)
    return total


def body(queries, key_in, values_in, skip_gain, filter_tap_bank, lag_slot):
    length, chan_width = key_in.shape
    slots_dev = filter_tap_bank.shape[0]
    cycle_steps = lag_slot.shape[0]
    group_dev = filter_tap_bank.shape[2] // lax.axis_size("sub")
    n_ctx = lax.axis_size("ctx")
    sub_index = lax.axis_index("sub")
    mixed_input = key_in * values_in
    fwd_real, fwd_imag, inv_real, inv_imag = lax.optimization_barrier(tables(length))
    members = chan_width // group_dev
    member_major = (
        mixed_input.reshape(length, group_dev, members).transpose(0, 2, 1).reshape(length, chan_width)
    )
    n_sub = lax.axis_size("sub")
    received = []
    for offset in range(n_sub):
        wanted = lax.dynamic_slice_in_dim(
            filter_tap_bank, ((sub_index + offset) % n_sub) * group_dev, group_dev, 2
        )
        if offset:
            wanted = lax.ppermute(
                wanted, "sub", [(i, (i + offset) % n_sub) for i in range(n_sub)]
            )
        received.append(wanted)
    received = jnp.stack(received)
    pieces = []
    for cycle_step in range(cycle_steps):
        slot_index = lag_slot[cycle_step]
        owner = slot_index // slots_dev
        source = (sub_index - owner % n_sub) % n_sub
        held_piece = received[source, slot_index % slots_dev]
        pieces.append(from_root(held_piece, "ctx", owner // n_sub))
    filter_taps = jnp.concatenate(pieces, axis=1)
    filter_spec = transform(filter_taps, fwd_real, fwd_imag, HIGHEST)
    row_sign = (
        1.0 - 2.0 * (lax.broadcasted_iota(jnp.int32, (length, 1), 0) % 2).astype(jnp.float32)
    )[None]
    segment_spec = [
        filter_spec[:, :, cycle_step * group_dev : (cycle_step + 1) * group_dev]
        for cycle_step in range(cycle_steps)
    ]
    effective = [row_sign * segment_spec[0]]
    for cycle_step in range(1, cycle_steps):
        effective.append(segment_spec[cycle_step - 1] + row_sign * segment_spec[cycle_step])
    effective.append(segment_spec[cycle_steps - 1])

    last_raw = max(n_ctx - 2, 0)
    raw_rounds = min(cycle_steps, last_raw)
    part_terms = min(cycle_steps, raw_rounds + 1)
    chunks = CHUNKS if members % CHUNKS == 0 else 1
    chunk_w = chan_width // chunks
    outs = []
    for chunk in range(chunks):
        cols = slice(chunk * chunk_w, (chunk + 1) * chunk_w)
        filters = effective
        moving = member_major[:, cols]
        blocks = [moving]
        for step in range(1, raw_rounds + 1):
            route = [(k, k + 1) for k in range(step - 1, last_raw)]
            moving = lax.ppermute(moving, "ctx", route)
            blocks.append(moving)
        specs = [transform(b, fwd_real, fwd_imag) for b in blocks]
        conv_out = inverse(filtered_sum(specs, filters), inv_real, inv_imag)
        if n_ctx >= 2:
            partial = inverse(
                filtered_sum(specs[:part_terms], filters[1 : part_terms + 1]), inv_real, inv_imag
            )
            conv_out = conv_out + lax.ppermute(partial, "ctx", [(last_raw, last_raw + 1)])
        outs.append(conv_out)
    conv_all = jnp.concatenate(outs, axis=1) if chunks > 1 else outs[0]
    conv_all = conv_all.reshape(length, members, group_dev).transpose(0, 2, 1).reshape(length, chan_width)
    return queries * (conv_all + skip_gain[None, :] * mixed_input)


def solution(mesh):
    in_specs = (
        P(("groups", "ctx"), ("chan", "sub")),
        P(("groups", "ctx"), ("chan", "sub")),
        P(("groups", "ctx"), ("chan", "sub")),
        P(("chan", "sub")),
        P(("ctx", "sub"), None, "chan"),
        P(),
    )
    out_specs = P(("groups", "ctx"), ("chan", "sub"))
    return jax.shard_map(body, mesh=mesh, in_specs=in_specs, out_specs=out_specs, check_vma=False)
```

```python
import jax
import jax.numpy as jnp
from jax import lax
from jax.sharding import PartitionSpec as P

HIGHEST = lax.Precision.HIGHEST
DATA_PRECISION = lax.Precision.HIGH
CHUNKS = 4


def from_root(block, axis, owner):
    block = jnp.where(lax.axis_index(axis) == owner, block, jnp.zeros_like(block))
    return lax.psum(block, axis)


def tables(length):
    freq_rows = lax.broadcasted_iota(jnp.int32, (length, length), 0)
    place_cols = lax.broadcasted_iota(jnp.int32, (length, length), 1)
    angle = jnp.pi * (freq_rows * place_cols % (2 * length)).astype(jnp.float32) / length
    parity = 1.0 - 2.0 * (place_cols % 2).astype(jnp.float32)
    fwd_real = jnp.cos(angle)
    fwd_imag = jnp.where(freq_rows == 0, parity, -jnp.sin(angle))
    out_place = freq_rows + length
    back_angle = jnp.pi * (place_cols * out_place % (2 * length)).astype(jnp.float32) / length
    out_parity = 1.0 - 2.0 * (out_place % 2).astype(jnp.float32)
    inv_real = jnp.where(place_cols == 0, 1.0, 2.0 * jnp.cos(back_angle)) / (2 * length)
    inv_imag = jnp.where(place_cols == 0, out_parity, -2.0 * jnp.sin(back_angle)) / (2 * length)
    return (fwd_real, fwd_imag, inv_real, inv_imag)


def transform(block, fwd_real, fwd_imag, precision=DATA_PRECISION):
    return jnp.stack(
        [jnp.dot(fwd_real, block, precision=precision), jnp.dot(fwd_imag, block, precision=precision)]
    )


def inverse(total, inv_real, inv_imag):
    return jnp.dot(inv_real, total[0], precision=DATA_PRECISION) + jnp.dot(
        inv_imag, total[1], precision=DATA_PRECISION
    )


def apply_filter(spectrum, filt):
    length = spectrum.shape[1]
    chan_width = spectrum.shape[2]
    group_dev = filt.shape[2]
    a_real = spectrum[0].reshape(length, chan_width // group_dev, group_dev)
    a_imag = spectrum[1].reshape(length, chan_width // group_dev, group_dev)
    e_real = filt[0][:, None, :]
    e_imag = filt[1][:, None, :]
    first_row = lax.broadcasted_iota(jnp.int32, (length, 1, 1), 0) == 0
    prod_real = jnp.where(first_row, a_real * e_real, a_real * e_real - a_imag * e_imag)
    prod_imag = jnp.where(first_row, a_imag * e_imag, a_real * e_imag + a_imag * e_real)
    return jnp.stack([prod_real.reshape(length, chan_width), prod_imag.reshape(length, chan_width)])


def filtered_sum(specs, filters):
    total = apply_filter(specs[0], filters[0])
    for spec, filt in zip(specs[1:], filters[1:]):
        total = total + apply_filter(spec, filt)
    return total


def body(queries, key_in, values_in, skip_gain, filter_tap_bank, lag_slot):
    length, chan_width = key_in.shape
    slots_dev = filter_tap_bank.shape[0]
    cycle_steps = lag_slot.shape[0]
    group_dev = filter_tap_bank.shape[2] // lax.axis_size("sub")
    n_ctx = lax.axis_size("ctx")
    sub_index = lax.axis_index("sub")
    fwd_real, fwd_imag, inv_real, inv_imag = lax.optimization_barrier(tables(length))
    members = chan_width // group_dev
    n_sub = lax.axis_size("sub")
    received = []
    for offset in range(n_sub):
        wanted = lax.dynamic_slice_in_dim(
            filter_tap_bank, ((sub_index + offset) % n_sub) * group_dev, group_dev, 2
        )
        if offset:
            wanted = lax.ppermute(
                wanted, "sub", [(i, (i + offset) % n_sub) for i in range(n_sub)]
            )
        received.append(wanted)
    received = jnp.stack(received)
    pieces = []
    for cycle_step in range(cycle_steps):
        slot_index = lag_slot[cycle_step]
        owner = slot_index // slots_dev
        source = (sub_index - owner % n_sub) % n_sub
        held_piece = received[source, slot_index % slots_dev]
        pieces.append(from_root(held_piece, "ctx", owner // n_sub))
    filter_taps = jnp.concatenate(pieces, axis=1)
    mixed_input = key_in * values_in
    member_major = (
        mixed_input.reshape(length, group_dev, members).transpose(0, 2, 1).reshape(length, chan_width)
    )
    row_sign = (
        1.0 - 2.0 * (lax.broadcasted_iota(jnp.int32, (length, 1), 0) % 2).astype(jnp.float32)
    )[None]

    last_raw = max(n_ctx - 2, 0)
    raw_rounds = min(cycle_steps, last_raw)
    part_terms = min(cycle_steps, raw_rounds + 1)
    chunks = CHUNKS if members % CHUNKS == 0 else 1
    chunk_w = chan_width // chunks
    outs = []
    arrived = None
    sent = None
    partials = []
    effective = None
    for chunk in range(chunks):
        cols = slice(chunk * chunk_w, (chunk + 1) * chunk_w)
        own = member_major[:, cols]
        if arrived is not None:
            own, _ = lax.optimization_barrier((own, arrived))
        blocks = [own]
        for distance in range(1, raw_rounds + 1):
            route = [(k - distance, k) for k in range(distance, last_raw + 1)]
            blocks.append(lax.ppermute(own, "ctx", route))
        arrived = blocks[1:] if raw_rounds else None
        if partials and raw_rounds:
            late, _ = lax.optimization_barrier((blocks[1:], partials[-1]))
            blocks = blocks[:1] + list(late)
        if effective is None:
            if arrived is not None:
                filter_taps, _ = lax.optimization_barrier((filter_taps, arrived))
            filter_spec = transform(filter_taps, fwd_real, fwd_imag, HIGHEST)
            segment_spec = [
                filter_spec[:, :, step * group_dev : (step + 1) * group_dev]
                for step in range(cycle_steps)
            ]
            effective = [row_sign * segment_spec[0]]
            for step in range(1, cycle_steps):
                effective.append(segment_spec[step - 1] + row_sign * segment_spec[step])
            effective.append(segment_spec[cycle_steps - 1])
        filters = effective
        specs = [transform(b, fwd_real, fwd_imag) for b in blocks]
        conv_out = inverse(filtered_sum(specs, filters), inv_real, inv_imag)
        if n_ctx >= 2:
            part_specs = specs[:part_terms]
            if sent is not None:
                part_specs, _ = lax.optimization_barrier((part_specs, sent))
            partial = inverse(
                filtered_sum(part_specs, filters[1 : part_terms + 1]), inv_real, inv_imag
            )
            partials.append(partial)
            sent = lax.ppermute(partial, "ctx", [(last_raw, last_raw + 1)])
            conv_out = conv_out + sent
        outs.append(conv_out)
    conv_all = jnp.concatenate(outs, axis=1) if chunks > 1 else outs[0]
    conv_all = conv_all.reshape(length, members, group_dev).transpose(0, 2, 1).reshape(length, chan_width)
    return queries * (conv_all + skip_gain[None, :] * mixed_input)


def solution(mesh):
    in_specs = (
        P(("groups", "ctx"), ("chan", "sub")),
        P(("groups", "ctx"), ("chan", "sub")),
        P(("groups", "ctx"), ("chan", "sub")),
        P(("chan", "sub")),
        P(("ctx", "sub"), None, "chan"),
        P(),
    )
    out_specs = P(("groups", "ctx"), ("chan", "sub"))
    return jax.shard_map(body, mesh=mesh, in_specs=in_specs, out_specs=out_specs, check_vma=False)
```

```python
import jax
import jax.numpy as jnp
from jax import lax
from jax.sharding import PartitionSpec as P

HIGHEST = lax.Precision.HIGHEST
DATA_PRECISION = lax.Precision.HIGH
CHUNKS = 4


def from_root(block, axis, owner):
    block = jnp.where(lax.axis_index(axis) == owner, block, jnp.zeros_like(block))
    return lax.psum(block, axis)


def tables(length):
    freq_rows = lax.broadcasted_iota(jnp.int32, (length, length), 0)
    place_cols = lax.broadcasted_iota(jnp.int32, (length, length), 1)
    angle = jnp.pi * (freq_rows * place_cols % (2 * length)).astype(jnp.float32) / length
    parity = 1.0 - 2.0 * (place_cols % 2).astype(jnp.float32)
    fwd_real = jnp.cos(angle)
    fwd_imag = jnp.where(freq_rows == 0, parity, -jnp.sin(angle))
    out_place = freq_rows + length
    back_angle = jnp.pi * (place_cols * out_place % (2 * length)).astype(jnp.float32) / length
    out_parity = 1.0 - 2.0 * (out_place % 2).astype(jnp.float32)
    inv_real = jnp.where(place_cols == 0, 1.0, 2.0 * jnp.cos(back_angle)) / (2 * length)
    inv_imag = jnp.where(place_cols == 0, out_parity, -2.0 * jnp.sin(back_angle)) / (2 * length)
    return (fwd_real, fwd_imag, inv_real, inv_imag)


def transform(block, fwd_real, fwd_imag, precision=DATA_PRECISION):
    return jnp.stack(
        [jnp.dot(fwd_real, block, precision=precision), jnp.dot(fwd_imag, block, precision=precision)]
    )


def inverse(total, inv_real, inv_imag):
    return jnp.dot(inv_real, total[0], precision=DATA_PRECISION) + jnp.dot(
        inv_imag, total[1], precision=DATA_PRECISION
    )


def apply_filter(spectrum, filt):
    length = spectrum.shape[1]
    chan_width = spectrum.shape[2]
    group_dev = filt.shape[2]
    a_real = spectrum[0].reshape(length, chan_width // group_dev, group_dev)
    a_imag = spectrum[1].reshape(length, chan_width // group_dev, group_dev)
    e_real = filt[0][:, None, :]
    e_imag = filt[1][:, None, :]
    first_row = lax.broadcasted_iota(jnp.int32, (length, 1, 1), 0) == 0
    prod_real = jnp.where(first_row, a_real * e_real, a_real * e_real - a_imag * e_imag)
    prod_imag = jnp.where(first_row, a_imag * e_imag, a_real * e_imag + a_imag * e_real)
    return jnp.stack([prod_real.reshape(length, chan_width), prod_imag.reshape(length, chan_width)])


def filtered_sum(specs, filters):
    total = apply_filter(specs[0], filters[0])
    for spec, filt in zip(specs[1:], filters[1:]):
        total = total + apply_filter(spec, filt)
    return total


def body(queries, key_in, values_in, skip_gain, filter_tap_bank, lag_slot):
    length, chan_width = key_in.shape
    slots_dev = filter_tap_bank.shape[0]
    cycle_steps = lag_slot.shape[0]
    group_dev = filter_tap_bank.shape[2] // lax.axis_size("sub")
    n_ctx = lax.axis_size("ctx")
    sub_index = lax.axis_index("sub")
    fwd_real, fwd_imag, inv_real, inv_imag = lax.optimization_barrier(tables(length))
    members = chan_width // group_dev
    n_sub = lax.axis_size("sub")
    received = []
    for offset in range(n_sub):
        wanted = lax.dynamic_slice_in_dim(
            filter_tap_bank, ((sub_index + offset) % n_sub) * group_dev, group_dev, 2
        )
        if offset:
            wanted = lax.ppermute(
                wanted, "sub", [(i, (i + offset) % n_sub) for i in range(n_sub)]
            )
        received.append(wanted)
    received = jnp.stack(received)
    pieces = []
    for cycle_step in range(cycle_steps):
        slot_index = lag_slot[cycle_step]
        owner = slot_index // slots_dev
        source = (sub_index - owner % n_sub) % n_sub
        held_piece = received[source, slot_index % slots_dev]
        pieces.append(from_root(held_piece, "ctx", owner // n_sub))
    filter_taps = jnp.concatenate(pieces, axis=1)
    key_in, values_in, filter_taps = lax.optimization_barrier((key_in, values_in, filter_taps))
    mixed_input = key_in * values_in
    member_major = (
        mixed_input.reshape(length, group_dev, members).transpose(0, 2, 1).reshape(length, chan_width)
    )
    row_sign = (
        1.0 - 2.0 * (lax.broadcasted_iota(jnp.int32, (length, 1), 0) % 2).astype(jnp.float32)
    )[None]

    last_raw = max(n_ctx - 2, 0)
    raw_rounds = min(cycle_steps, last_raw)
    part_terms = min(cycle_steps, raw_rounds + 1)
    chunks = CHUNKS if members % CHUNKS == 0 else 1
    chunk_w = chan_width // chunks
    outs = []
    arrived = None
    sent = None
    partials = []
    effective = None
    for chunk in range(chunks):
        cols = slice(chunk * chunk_w, (chunk + 1) * chunk_w)
        own = member_major[:, cols]
        if arrived is not None:
            own, _ = lax.optimization_barrier((own, arrived))
        blocks = [own]
        for distance in range(1, raw_rounds + 1):
            route = [(k - distance, k) for k in range(distance, last_raw + 1)]
            blocks.append(lax.ppermute(own, "ctx", route))
        arrived = blocks[1:] if raw_rounds else None
        if partials and raw_rounds:
            late, _ = lax.optimization_barrier((blocks[1:], partials[-1]))
            blocks = blocks[:1] + list(late)
        if effective is None:
            filter_spec = transform(filter_taps, fwd_real, fwd_imag, HIGHEST)
            segment_spec = [
                filter_spec[:, :, step * group_dev : (step + 1) * group_dev]
                for step in range(cycle_steps)
            ]
            effective = [row_sign * segment_spec[0]]
            for step in range(1, cycle_steps):
                effective.append(segment_spec[step - 1] + row_sign * segment_spec[step])
            effective.append(segment_spec[cycle_steps - 1])
        filters = effective
        specs = [transform(b, fwd_real, fwd_imag) for b in blocks]
        conv_out = inverse(filtered_sum(specs, filters), inv_real, inv_imag)
        if n_ctx >= 2:
            part_specs = specs[:part_terms]
            if sent is not None:
                part_specs, _ = lax.optimization_barrier((part_specs, sent))
            partial = inverse(
                filtered_sum(part_specs, filters[1 : part_terms + 1]), inv_real, inv_imag
            )
            partials.append(partial)
            sent = lax.ppermute(partial, "ctx", [(last_raw, last_raw + 1)])
            conv_out = conv_out + sent
        outs.append(conv_out)
    conv_all = jnp.concatenate(outs, axis=1) if chunks > 1 else outs[0]
    conv_all = conv_all.reshape(length, members, group_dev).transpose(0, 2, 1).reshape(length, chan_width)
    return queries * (conv_all + skip_gain[None, :] * mixed_input)


def solution(mesh):
    in_specs = (
        P(("groups", "ctx"), ("chan", "sub")),
        P(("groups", "ctx"), ("chan", "sub")),
        P(("groups", "ctx"), ("chan", "sub")),
        P(("chan", "sub")),
        P(("ctx", "sub"), None, "chan"),
        P(),
    )
    out_specs = P(("groups", "ctx"), ("chan", "sub"))
    return jax.shard_map(body, mesh=mesh, in_specs=in_specs, out_specs=out_specs, check_vma=False)
```

```python
import jax
import jax.numpy as jnp
from jax import lax
from jax.sharding import PartitionSpec as P

HIGHEST = lax.Precision.HIGHEST
DATA_PRECISION = lax.Precision.HIGH
CHUNKS = 4


def from_root(block, axis, owner):
    block = jnp.where(lax.axis_index(axis) == owner, block, jnp.zeros_like(block))
    return lax.psum(block, axis)


def tables(length):
    freq_rows = lax.broadcasted_iota(jnp.int32, (length, length), 0)
    place_cols = lax.broadcasted_iota(jnp.int32, (length, length), 1)
    angle = jnp.pi * (freq_rows * place_cols % (2 * length)).astype(jnp.float32) / length
    parity = 1.0 - 2.0 * (place_cols % 2).astype(jnp.float32)
    fwd_real = jnp.cos(angle)
    fwd_imag = jnp.where(freq_rows == 0, parity, -jnp.sin(angle))
    out_place = freq_rows + length
    back_angle = jnp.pi * (place_cols * out_place % (2 * length)).astype(jnp.float32) / length
    out_parity = 1.0 - 2.0 * (out_place % 2).astype(jnp.float32)
    inv_real = jnp.where(place_cols == 0, 1.0, 2.0 * jnp.cos(back_angle)) / (2 * length)
    inv_imag = jnp.where(place_cols == 0, out_parity, -2.0 * jnp.sin(back_angle)) / (2 * length)
    return (fwd_real, fwd_imag, inv_real, inv_imag)


def transform(block, fwd_real, fwd_imag, precision=DATA_PRECISION):
    return jnp.stack(
        [jnp.dot(fwd_real, block, precision=precision), jnp.dot(fwd_imag, block, precision=precision)]
    )


def inverse(total, inv_real, inv_imag):
    return jnp.dot(inv_real, total[0], precision=DATA_PRECISION) + jnp.dot(
        inv_imag, total[1], precision=DATA_PRECISION
    )


def apply_filter(spectrum, filt):
    length = spectrum.shape[1]
    chan_width = spectrum.shape[2]
    group_dev = filt.shape[2]
    a_real = spectrum[0].reshape(length, chan_width // group_dev, group_dev)
    a_imag = spectrum[1].reshape(length, chan_width // group_dev, group_dev)
    e_real = filt[0][:, None, :]
    e_imag = filt[1][:, None, :]
    first_row = lax.broadcasted_iota(jnp.int32, (length, 1, 1), 0) == 0
    prod_real = jnp.where(first_row, a_real * e_real, a_real * e_real - a_imag * e_imag)
    prod_imag = jnp.where(first_row, a_imag * e_imag, a_real * e_imag + a_imag * e_real)
    return jnp.stack([prod_real.reshape(length, chan_width), prod_imag.reshape(length, chan_width)])


def filtered_sum(specs, filters):
    total = apply_filter(specs[0], filters[0])
    for spec, filt in zip(specs[1:], filters[1:]):
        total = total + apply_filter(spec, filt)
    return total


def body(queries, key_in, values_in, skip_gain, filter_tap_bank, lag_slot):
    length, chan_width = key_in.shape
    slots_dev = filter_tap_bank.shape[0]
    cycle_steps = lag_slot.shape[0]
    group_dev = filter_tap_bank.shape[2] // lax.axis_size("sub")
    n_ctx = lax.axis_size("ctx")
    sub_index = lax.axis_index("sub")
    mixed_input = key_in * values_in
    fwd_real, fwd_imag, inv_real, inv_imag = lax.optimization_barrier(tables(length))
    members = chan_width // group_dev
    member_major = (
        mixed_input.reshape(length, group_dev, members).transpose(0, 2, 1).reshape(length, chan_width)
    )
    n_sub = lax.axis_size("sub")
    received = []
    for offset in range(n_sub):
        wanted = lax.dynamic_slice_in_dim(
            filter_tap_bank, ((sub_index + offset) % n_sub) * group_dev, group_dev, 2
        )
        if offset:
            wanted = lax.ppermute(
                wanted, "sub", [(i, (i + offset) % n_sub) for i in range(n_sub)]
            )
        received.append(wanted)
    received = jnp.stack(received)
    pieces = []
    for cycle_step in range(cycle_steps):
        slot_index = lag_slot[cycle_step]
        owner = slot_index // slots_dev
        source = (sub_index - owner % n_sub) % n_sub
        held_piece = received[source, slot_index % slots_dev]
        pieces.append(from_root(held_piece, "ctx", owner // n_sub))
    filter_taps = jnp.concatenate(pieces, axis=1)
    filter_spec = transform(filter_taps, fwd_real, fwd_imag, HIGHEST)
    row_sign = (
        1.0 - 2.0 * (lax.broadcasted_iota(jnp.int32, (length, 1), 0) % 2).astype(jnp.float32)
    )[None]
    segment_spec = [
        filter_spec[:, :, cycle_step * group_dev : (cycle_step + 1) * group_dev]
        for cycle_step in range(cycle_steps)
    ]
    effective = [row_sign * segment_spec[0]]
    for cycle_step in range(1, cycle_steps):
        effective.append(segment_spec[cycle_step - 1] + row_sign * segment_spec[cycle_step])
    effective.append(segment_spec[cycle_steps - 1])

    last_raw = max(n_ctx - 2, 0)
    raw_rounds = min(cycle_steps, last_raw)
    part_terms = min(cycle_steps, raw_rounds + 1)
    chunks = CHUNKS if members % CHUNKS == 0 else 1
    chunk_w = chan_width // chunks
    outs = []
    last_round = None
    partial = None
    sent = None
    for chunk in range(chunks):
        cols = slice(chunk * chunk_w, (chunk + 1) * chunk_w)
        filters = effective
        moving = member_major[:, cols]
        blocks = [moving]
        for step in range(1, raw_rounds + 1):
            route = [(k, k + 1) for k in range(step - 1, last_raw)]
            if step == raw_rounds and step > 1 and last_round is not None:
                moving, _ = lax.optimization_barrier((moving, last_round))
            moving = lax.ppermute(moving, "ctx", route)
            if step == raw_rounds and step > 1 and partial is not None:
                moving, _ = lax.optimization_barrier((moving, partial))
            blocks.append(moving)
        if raw_rounds > 1:
            last_round = blocks[-1]
        specs = [transform(b, fwd_real, fwd_imag) for b in blocks]
        conv_out = inverse(filtered_sum(specs, filters), inv_real, inv_imag)
        if n_ctx >= 2:
            part_specs = specs[:part_terms]
            if sent is not None:
                part_specs, _ = lax.optimization_barrier((part_specs, sent))
            partial = inverse(
                filtered_sum(part_specs, filters[1 : part_terms + 1]), inv_real, inv_imag
            )
            sent = lax.ppermute(partial, "ctx", [(last_raw, last_raw + 1)])
            conv_out = conv_out + sent
        outs.append(conv_out)
    conv_all = jnp.concatenate(outs, axis=1) if chunks > 1 else outs[0]
    conv_all = conv_all.reshape(length, members, group_dev).transpose(0, 2, 1).reshape(length, chan_width)
    return queries * (conv_all + skip_gain[None, :] * mixed_input)


def solution(mesh):
    in_specs = (
        P(("groups", "ctx"), ("chan", "sub")),
        P(("groups", "ctx"), ("chan", "sub")),
        P(("groups", "ctx"), ("chan", "sub")),
        P(("chan", "sub")),
        P(("ctx", "sub"), None, "chan"),
        P(),
    )
    out_specs = P(("groups", "ctx"), ("chan", "sub"))
    return jax.shard_map(body, mesh=mesh, in_specs=in_specs, out_specs=out_specs, check_vma=False)
```

```python
import jax
import jax.numpy as jnp
from jax import lax
from jax.sharding import PartitionSpec as P

HIGHEST = lax.Precision.HIGHEST
DATA_PRECISION = lax.Precision.HIGH
CHUNKS = 4


def from_root(block, axis, owner):
    block = jnp.where(lax.axis_index(axis) == owner, block, jnp.zeros_like(block))
    return lax.psum(block, axis)


def tables(length):
    freq_rows = lax.broadcasted_iota(jnp.int32, (length, length), 0)
    place_cols = lax.broadcasted_iota(jnp.int32, (length, length), 1)
    angle = jnp.pi * (freq_rows * place_cols % (2 * length)).astype(jnp.float32) / length
    parity = 1.0 - 2.0 * (place_cols % 2).astype(jnp.float32)
    fwd_real = jnp.cos(angle)
    fwd_imag = jnp.where(freq_rows == 0, parity, -jnp.sin(angle))
    out_place = freq_rows + length
    back_angle = jnp.pi * (place_cols * out_place % (2 * length)).astype(jnp.float32) / length
    out_parity = 1.0 - 2.0 * (out_place % 2).astype(jnp.float32)
    inv_real = jnp.where(place_cols == 0, 1.0, 2.0 * jnp.cos(back_angle)) / (2 * length)
    inv_imag = jnp.where(place_cols == 0, out_parity, -2.0 * jnp.sin(back_angle)) / (2 * length)
    return (fwd_real, fwd_imag, inv_real, inv_imag)


def transform(block, fwd_real, fwd_imag, precision=DATA_PRECISION):
    return jnp.stack(
        [jnp.dot(fwd_real, block, precision=precision), jnp.dot(fwd_imag, block, precision=precision)]
    )


def inverse(total, inv_real, inv_imag):
    return jnp.dot(inv_real, total[0], precision=DATA_PRECISION) + jnp.dot(
        inv_imag, total[1], precision=DATA_PRECISION
    )


def apply_filter(spectrum, filt):
    length = spectrum.shape[1]
    chan_width = spectrum.shape[2]
    group_dev = filt.shape[2]
    a_real = spectrum[0].reshape(length, chan_width // group_dev, group_dev)
    a_imag = spectrum[1].reshape(length, chan_width // group_dev, group_dev)
    e_real = filt[0][:, None, :]
    e_imag = filt[1][:, None, :]
    first_row = lax.broadcasted_iota(jnp.int32, (length, 1, 1), 0) == 0
    prod_real = jnp.where(first_row, a_real * e_real, a_real * e_real - a_imag * e_imag)
    prod_imag = jnp.where(first_row, a_imag * e_imag, a_real * e_imag + a_imag * e_real)
    return jnp.stack([prod_real.reshape(length, chan_width), prod_imag.reshape(length, chan_width)])


def filtered_sum(specs, filters):
    total = apply_filter(specs[0], filters[0])
    for spec, filt in zip(specs[1:], filters[1:]):
        total = total + apply_filter(spec, filt)
    return total


def body(queries, key_in, values_in, skip_gain, filter_tap_bank, lag_slot):
    length, chan_width = key_in.shape
    slots_dev = filter_tap_bank.shape[0]
    cycle_steps = lag_slot.shape[0]
    group_dev = filter_tap_bank.shape[2] // lax.axis_size("sub")
    n_ctx = lax.axis_size("ctx")
    sub_index = lax.axis_index("sub")
    mixed_input = key_in * values_in
    fwd_real, fwd_imag, inv_real, inv_imag = lax.optimization_barrier(tables(length))
    members = chan_width // group_dev
    member_major = (
        mixed_input.reshape(length, group_dev, members).transpose(0, 2, 1).reshape(length, chan_width)
    )
    n_sub = lax.axis_size("sub")
    received = []
    for offset in range(n_sub):
        wanted = lax.dynamic_slice_in_dim(
            filter_tap_bank, ((sub_index + offset) % n_sub) * group_dev, group_dev, 2
        )
        if offset:
            wanted = lax.ppermute(
                wanted, "sub", [(i, (i + offset) % n_sub) for i in range(n_sub)]
            )
        received.append(wanted)
    received = jnp.stack(received)
    gathered = lax.all_gather(received, "ctx")
    pieces = []
    for cycle_step in range(cycle_steps):
        slot_index = lag_slot[cycle_step]
        owner = slot_index // slots_dev
        source = (sub_index - owner % n_sub) % n_sub
        pieces.append(gathered[owner // n_sub, source, slot_index % slots_dev])
    filter_taps = jnp.concatenate(pieces, axis=1)
    filter_spec = transform(filter_taps, fwd_real, fwd_imag, HIGHEST)
    row_sign = (
        1.0 - 2.0 * (lax.broadcasted_iota(jnp.int32, (length, 1), 0) % 2).astype(jnp.float32)
    )[None]
    segment_spec = [
        filter_spec[:, :, cycle_step * group_dev : (cycle_step + 1) * group_dev]
        for cycle_step in range(cycle_steps)
    ]
    effective = [row_sign * segment_spec[0]]
    for cycle_step in range(1, cycle_steps):
        effective.append(segment_spec[cycle_step - 1] + row_sign * segment_spec[cycle_step])
    effective.append(segment_spec[cycle_steps - 1])

    last_raw = max(n_ctx - 2, 0)
    raw_rounds = min(cycle_steps, last_raw)
    part_terms = min(cycle_steps, raw_rounds + 1)
    chunks = CHUNKS if members % CHUNKS == 0 else 1
    chunk_w = chan_width // chunks
    outs = []
    last_round = None
    partial = None
    sent = None
    for chunk in range(chunks):
        cols = slice(chunk * chunk_w, (chunk + 1) * chunk_w)
        filters = effective
        moving = member_major[:, cols]
        blocks = [moving]
        for step in range(1, raw_rounds + 1):
            route = [(k, k + 1) for k in range(step - 1, last_raw)]
            if step == raw_rounds and step > 1 and last_round is not None:
                moving, _ = lax.optimization_barrier((moving, last_round))
            moving = lax.ppermute(moving, "ctx", route)
            if step == raw_rounds and step > 1 and partial is not None:
                moving, _ = lax.optimization_barrier((moving, partial))
            blocks.append(moving)
        if raw_rounds > 1:
            last_round = blocks[-1]
        specs = [transform(b, fwd_real, fwd_imag) for b in blocks]
        conv_out = inverse(filtered_sum(specs, filters), inv_real, inv_imag)
        if n_ctx >= 2:
            part_specs = specs[:part_terms]
            if sent is not None:
                part_specs, _ = lax.optimization_barrier((part_specs, sent))
            partial = inverse(
                filtered_sum(part_specs, filters[1 : part_terms + 1]), inv_real, inv_imag
            )
            sent = lax.ppermute(partial, "ctx", [(last_raw, last_raw + 1)])
            conv_out = conv_out + sent
        outs.append(conv_out)
    conv_all = jnp.concatenate(outs, axis=1) if chunks > 1 else outs[0]
    conv_all = conv_all.reshape(length, members, group_dev).transpose(0, 2, 1).reshape(length, chan_width)
    return queries * (conv_all + skip_gain[None, :] * mixed_input)


def solution(mesh):
    in_specs = (
        P(("groups", "ctx"), ("chan", "sub")),
        P(("groups", "ctx"), ("chan", "sub")),
        P(("groups", "ctx"), ("chan", "sub")),
        P(("chan", "sub")),
        P(("ctx", "sub"), None, "chan"),
        P(),
    )
    out_specs = P(("groups", "ctx"), ("chan", "sub"))
    return jax.shard_map(body, mesh=mesh, in_specs=in_specs, out_specs=out_specs, check_vma=False)
```

```python
import jax
import jax.numpy as jnp
from jax import lax
from jax.sharding import PartitionSpec as P

HIGHEST = lax.Precision.HIGHEST
DATA_PRECISION = lax.Precision.HIGH
CHUNKS = 2


def from_root(block, axis, owner):
    block = jnp.where(lax.axis_index(axis) == owner, block, jnp.zeros_like(block))
    return lax.psum(block, axis)


def tables(length):
    freq_rows = lax.broadcasted_iota(jnp.int32, (length, length), 0)
    place_cols = lax.broadcasted_iota(jnp.int32, (length, length), 1)
    angle = jnp.pi * (freq_rows * place_cols % (2 * length)).astype(jnp.float32) / length
    parity = 1.0 - 2.0 * (place_cols % 2).astype(jnp.float32)
    fwd_real = jnp.cos(angle)
    fwd_imag = jnp.where(freq_rows == 0, parity, -jnp.sin(angle))
    out_place = freq_rows + length
    back_angle = jnp.pi * (place_cols * out_place % (2 * length)).astype(jnp.float32) / length
    out_parity = 1.0 - 2.0 * (out_place % 2).astype(jnp.float32)
    inv_real = jnp.where(place_cols == 0, 1.0, 2.0 * jnp.cos(back_angle)) / (2 * length)
    inv_imag = jnp.where(place_cols == 0, out_parity, -2.0 * jnp.sin(back_angle)) / (2 * length)
    return (fwd_real, fwd_imag, inv_real, inv_imag)


def transform(block, fwd_real, fwd_imag, precision=DATA_PRECISION):
    return jnp.stack(
        [jnp.dot(fwd_real, block, precision=precision), jnp.dot(fwd_imag, block, precision=precision)]
    )


def inverse(total, inv_real, inv_imag):
    return jnp.dot(inv_real, total[0], precision=DATA_PRECISION) + jnp.dot(
        inv_imag, total[1], precision=DATA_PRECISION
    )


def apply_filter(spectrum, filt):
    length = spectrum.shape[1]
    chan_width = spectrum.shape[2]
    group_dev = filt.shape[2]
    a_real = spectrum[0].reshape(length, chan_width // group_dev, group_dev)
    a_imag = spectrum[1].reshape(length, chan_width // group_dev, group_dev)
    e_real = filt[0][:, None, :]
    e_imag = filt[1][:, None, :]
    first_row = lax.broadcasted_iota(jnp.int32, (length, 1, 1), 0) == 0
    prod_real = jnp.where(first_row, a_real * e_real, a_real * e_real - a_imag * e_imag)
    prod_imag = jnp.where(first_row, a_imag * e_imag, a_real * e_imag + a_imag * e_real)
    return jnp.stack([prod_real.reshape(length, chan_width), prod_imag.reshape(length, chan_width)])


def filtered_sum(specs, filters):
    total = apply_filter(specs[0], filters[0])
    for spec, filt in zip(specs[1:], filters[1:]):
        total = total + apply_filter(spec, filt)
    return total


def body(queries, key_in, values_in, skip_gain, filter_tap_bank, lag_slot):
    length, chan_width = key_in.shape
    slots_dev = filter_tap_bank.shape[0]
    cycle_steps = lag_slot.shape[0]
    group_dev = filter_tap_bank.shape[2] // lax.axis_size("sub")
    n_ctx = lax.axis_size("ctx")
    sub_index = lax.axis_index("sub")
    mixed_input = key_in * values_in
    fwd_real, fwd_imag, inv_real, inv_imag = lax.optimization_barrier(tables(length))
    members = chan_width // group_dev
    member_major = (
        mixed_input.reshape(length, group_dev, members).transpose(0, 2, 1).reshape(length, chan_width)
    )
    n_sub = lax.axis_size("sub")
    received = []
    for offset in range(n_sub):
        wanted = lax.dynamic_slice_in_dim(
            filter_tap_bank, ((sub_index + offset) % n_sub) * group_dev, group_dev, 2
        )
        if offset:
            wanted = lax.ppermute(
                wanted, "sub", [(i, (i + offset) % n_sub) for i in range(n_sub)]
            )
        received.append(wanted)
    received = jnp.stack(received)
    pieces = []
    for cycle_step in range(cycle_steps):
        slot_index = lag_slot[cycle_step]
        owner = slot_index // slots_dev
        source = (sub_index - owner % n_sub) % n_sub
        held_piece = received[source, slot_index % slots_dev]
        pieces.append(from_root(held_piece, "ctx", owner // n_sub))
    filter_taps = jnp.concatenate(pieces, axis=1)
    filter_spec = transform(filter_taps, fwd_real, fwd_imag, HIGHEST)
    row_sign = (
        1.0 - 2.0 * (lax.broadcasted_iota(jnp.int32, (length, 1), 0) % 2).astype(jnp.float32)
    )[None]
    segment_spec = [
        filter_spec[:, :, cycle_step * group_dev : (cycle_step + 1) * group_dev]
        for cycle_step in range(cycle_steps)
    ]
    effective = [row_sign * segment_spec[0]]
    for cycle_step in range(1, cycle_steps):
        effective.append(segment_spec[cycle_step - 1] + row_sign * segment_spec[cycle_step])
    effective.append(segment_spec[cycle_steps - 1])

    last_raw = max(n_ctx - 2, 0)
    raw_rounds = min(cycle_steps, last_raw)
    part_terms = min(cycle_steps, raw_rounds + 1)
    chunks = CHUNKS if members % CHUNKS == 0 else 1
    chunk_w = chan_width // chunks
    outs = []
    last_round = None
    partial = None
    sent = None
    for chunk in range(chunks):
        cols = slice(chunk * chunk_w, (chunk + 1) * chunk_w)
        filters = effective
        moving = member_major[:, cols]
        blocks = [moving]
        for step in range(1, raw_rounds + 1):
            route = [(k, k + 1) for k in range(step - 1, last_raw)]
            if step == raw_rounds and step > 1 and last_round is not None:
                moving, _ = lax.optimization_barrier((moving, last_round))
            moving = lax.ppermute(moving, "ctx", route)
            if step == raw_rounds and step > 1 and partial is not None:
                moving, _ = lax.optimization_barrier((moving, partial))
            blocks.append(moving)
        if raw_rounds > 1:
            last_round = blocks[-1]
        specs = [transform(b, fwd_real, fwd_imag) for b in blocks]
        conv_out = inverse(filtered_sum(specs, filters), inv_real, inv_imag)
        if n_ctx >= 2:
            part_specs = specs[:part_terms]
            if sent is not None:
                part_specs, _ = lax.optimization_barrier((part_specs, sent))
            partial = inverse(
                filtered_sum(part_specs, filters[1 : part_terms + 1]), inv_real, inv_imag
            )
            sent = lax.ppermute(partial, "ctx", [(last_raw, last_raw + 1)])
            conv_out = conv_out + sent
        outs.append(conv_out)
    conv_all = jnp.concatenate(outs, axis=1) if chunks > 1 else outs[0]
    conv_all = conv_all.reshape(length, members, group_dev).transpose(0, 2, 1).reshape(length, chan_width)
    return queries * (conv_all + skip_gain[None, :] * mixed_input)


def solution(mesh):
    in_specs = (
        P(("groups", "ctx"), ("chan", "sub")),
        P(("groups", "ctx"), ("chan", "sub")),
        P(("groups", "ctx"), ("chan", "sub")),
        P(("chan", "sub")),
        P(("ctx", "sub"), None, "chan"),
        P(),
    )
    out_specs = P(("groups", "ctx"), ("chan", "sub"))
    return jax.shard_map(body, mesh=mesh, in_specs=in_specs, out_specs=out_specs, check_vma=False)
```

```python
import jax
import jax.numpy as jnp
from jax import lax
from jax.sharding import PartitionSpec as P

HIGHEST = lax.Precision.HIGHEST
DATA_PRECISION = lax.Precision.HIGH
CHUNKS = 4


def from_root(block, axis, owner):
    block = jnp.where(lax.axis_index(axis) == owner, block, jnp.zeros_like(block))
    return lax.psum(block, axis)


def tables(length):
    freq_rows = lax.broadcasted_iota(jnp.int32, (length, length), 0)
    place_cols = lax.broadcasted_iota(jnp.int32, (length, length), 1)
    angle = jnp.pi * (freq_rows * place_cols % (2 * length)).astype(jnp.float32) / length
    parity = 1.0 - 2.0 * (place_cols % 2).astype(jnp.float32)
    fwd_real = jnp.cos(angle)
    fwd_imag = jnp.where(freq_rows == 0, parity, -jnp.sin(angle))
    out_place = freq_rows + length
    back_angle = jnp.pi * (place_cols * out_place % (2 * length)).astype(jnp.float32) / length
    out_parity = 1.0 - 2.0 * (out_place % 2).astype(jnp.float32)
    inv_real = jnp.where(place_cols == 0, 1.0, 2.0 * jnp.cos(back_angle)) / (2 * length)
    inv_imag = jnp.where(place_cols == 0, out_parity, -2.0 * jnp.sin(back_angle)) / (2 * length)
    return (fwd_real, fwd_imag, inv_real, inv_imag)


def transform(block, fwd_real, fwd_imag, precision=DATA_PRECISION):
    return jnp.stack(
        [jnp.dot(fwd_real, block, precision=precision), jnp.dot(fwd_imag, block, precision=precision)]
    )


def transform_rows(block, fwd_real, fwd_imag):
    return jnp.stack(
        [
            jnp.einsum("pc,fp->cf", block, fwd_real, precision=DATA_PRECISION),
            jnp.einsum("pc,fp->cf", block, fwd_imag, precision=DATA_PRECISION),
        ]
    )


def inverse_rows(total, inv_real, inv_imag):
    return jnp.einsum("tf,cf->tc", inv_real, total[0], precision=DATA_PRECISION) + jnp.einsum(
        "tf,cf->tc", inv_imag, total[1], precision=DATA_PRECISION
    )


def apply_filter(spectrum, filt):
    chan_width = spectrum.shape[1]
    length = spectrum.shape[2]
    group_dev = filt.shape[1]
    a_real = spectrum[0].reshape(group_dev, chan_width // group_dev, length)
    a_imag = spectrum[1].reshape(group_dev, chan_width // group_dev, length)
    e_real = filt[0][:, None, :]
    e_imag = filt[1][:, None, :]
    first_col = lax.broadcasted_iota(jnp.int32, (1, 1, length), 2) == 0
    prod_real = jnp.where(first_col, a_real * e_real, a_real * e_real - a_imag * e_imag)
    prod_imag = jnp.where(first_col, a_imag * e_imag, a_real * e_imag + a_imag * e_real)
    return jnp.stack([prod_real.reshape(chan_width, length), prod_imag.reshape(chan_width, length)])


def filtered_sum(specs, filters):
    total = apply_filter(specs[0], filters[0])
    for spec, filt in zip(specs[1:], filters[1:]):
        total = total + apply_filter(spec, filt)
    return total


def body(queries, key_in, values_in, skip_gain, filter_tap_bank, lag_slot):
    length, chan_width = key_in.shape
    slots_dev = filter_tap_bank.shape[0]
    cycle_steps = lag_slot.shape[0]
    group_dev = filter_tap_bank.shape[2] // lax.axis_size("sub")
    n_ctx = lax.axis_size("ctx")
    sub_index = lax.axis_index("sub")
    mixed_input = key_in * values_in
    fwd_real, fwd_imag, inv_real, inv_imag = lax.optimization_barrier(tables(length))
    members = chan_width // group_dev
    n_sub = lax.axis_size("sub")
    received = []
    for offset in range(n_sub):
        wanted = lax.dynamic_slice_in_dim(
            filter_tap_bank, ((sub_index + offset) % n_sub) * group_dev, group_dev, 2
        )
        if offset:
            wanted = lax.ppermute(
                wanted, "sub", [(i, (i + offset) % n_sub) for i in range(n_sub)]
            )
        received.append(wanted)
    received = jnp.stack(received)
    pieces = []
    for cycle_step in range(cycle_steps):
        slot_index = lag_slot[cycle_step]
        owner = slot_index // slots_dev
        source = (sub_index - owner % n_sub) % n_sub
        held_piece = received[source, slot_index % slots_dev]
        pieces.append(from_root(held_piece, "ctx", owner // n_sub))
    filter_taps = jnp.concatenate(pieces, axis=1)
    filter_spec = transform(filter_taps, fwd_real, fwd_imag, HIGHEST)
    row_sign = (
        1.0 - 2.0 * (lax.broadcasted_iota(jnp.int32, (length, 1), 0) % 2).astype(jnp.float32)
    )[None]
    segment_spec = [
        filter_spec[:, :, cycle_step * group_dev : (cycle_step + 1) * group_dev]
        for cycle_step in range(cycle_steps)
    ]
    effective = [row_sign * segment_spec[0]]
    for cycle_step in range(1, cycle_steps):
        effective.append(segment_spec[cycle_step - 1] + row_sign * segment_spec[cycle_step])
    effective.append(segment_spec[cycle_steps - 1])
    effective = [e.transpose(0, 2, 1) for e in effective]

    last_raw = max(n_ctx - 2, 0)
    raw_rounds = min(cycle_steps, last_raw)
    part_terms = min(cycle_steps, raw_rounds + 1)
    chunks = CHUNKS if group_dev % CHUNKS == 0 else 1
    chunk_w = chan_width // chunks
    chunk_g = group_dev // chunks
    outs = []
    last_round = None
    partial = None
    sent = None
    for chunk in range(chunks):
        cols = slice(chunk * chunk_w, (chunk + 1) * chunk_w)
        filters = [e[:, chunk * chunk_g : (chunk + 1) * chunk_g] for e in effective]
        moving = mixed_input[:, cols]
        blocks = [moving]
        for step in range(1, raw_rounds + 1):
            route = [(k, k + 1) for k in range(step - 1, last_raw)]
            if step == raw_rounds and step > 1 and last_round is not None:
                moving, _ = lax.optimization_barrier((moving, last_round))
            moving = lax.ppermute(moving, "ctx", route)
            if step == raw_rounds and step > 1 and partial is not None:
                moving, _ = lax.optimization_barrier((moving, partial))
            blocks.append(moving)
        if raw_rounds > 1:
            last_round = blocks[-1]
        specs = [transform_rows(b, fwd_real, fwd_imag) for b in blocks]
        conv_out = inverse_rows(filtered_sum(specs, filters), inv_real, inv_imag)
        if n_ctx >= 2:
            part_specs = specs[:part_terms]
            if sent is not None:
                part_specs, _ = lax.optimization_barrier((part_specs, sent))
            partial = inverse_rows(
                filtered_sum(part_specs, filters[1 : part_terms + 1]), inv_real, inv_imag
            )
            sent = lax.ppermute(partial, "ctx", [(last_raw, last_raw + 1)])
            conv_out = conv_out + sent
        outs.append(conv_out)
    conv_all = jnp.concatenate(outs, axis=1) if chunks > 1 else outs[0]
    return queries * (conv_all + skip_gain[None, :] * mixed_input)


def solution(mesh):
    in_specs = (
        P(("groups", "ctx"), ("chan", "sub")),
        P(("groups", "ctx"), ("chan", "sub")),
        P(("groups", "ctx"), ("chan", "sub")),
        P(("chan", "sub")),
        P(("ctx", "sub"), None, "chan"),
        P(),
    )
    out_specs = P(("groups", "ctx"), ("chan", "sub"))
    return jax.shard_map(body, mesh=mesh, in_specs=in_specs, out_specs=out_specs, check_vma=False)
```

```python
import jax
import jax.numpy as jnp
from jax import lax
from jax.sharding import PartitionSpec as P

HIGHEST = lax.Precision.HIGHEST
DATA_PRECISION = lax.Precision.HIGH
CHUNKS = 4


def from_root(block, axis, owner):
    block = jnp.where(lax.axis_index(axis) == owner, block, jnp.zeros_like(block))
    return lax.psum(block, axis)


def tables(length):
    freq_rows = lax.broadcasted_iota(jnp.int32, (length, length), 0)
    place_cols = lax.broadcasted_iota(jnp.int32, (length, length), 1)
    angle = jnp.pi * (freq_rows * place_cols % (2 * length)).astype(jnp.float32) / length
    parity = 1.0 - 2.0 * (place_cols % 2).astype(jnp.float32)
    fwd_real = jnp.cos(angle)
    fwd_imag = jnp.where(freq_rows == 0, parity, -jnp.sin(angle))
    out_place = freq_rows + length
    back_angle = jnp.pi * (place_cols * out_place % (2 * length)).astype(jnp.float32) / length
    out_parity = 1.0 - 2.0 * (out_place % 2).astype(jnp.float32)
    inv_real = jnp.where(place_cols == 0, 1.0, 2.0 * jnp.cos(back_angle)) / (2 * length)
    inv_imag = jnp.where(place_cols == 0, out_parity, -2.0 * jnp.sin(back_angle)) / (2 * length)
    return (fwd_real, fwd_imag, inv_real, inv_imag)


def transform(block, fwd_real, fwd_imag, precision=DATA_PRECISION):
    return jnp.stack(
        [jnp.dot(fwd_real, block, precision=precision), jnp.dot(fwd_imag, block, precision=precision)]
    )


def transform_rows(block, fwd_real, fwd_imag):
    return jnp.stack(
        [
            jnp.einsum("pc,fp->cf", block, fwd_real, precision=DATA_PRECISION),
            jnp.einsum("pc,fp->cf", block, fwd_imag, precision=DATA_PRECISION),
        ]
    )


def inverse_rows(total, inv_real, inv_imag):
    return jnp.einsum("tf,cf->tc", inv_real, total[0], precision=DATA_PRECISION) + jnp.einsum(
        "tf,cf->tc", inv_imag, total[1], precision=DATA_PRECISION
    )


def apply_filter(spectrum, filt):
    chan_width = spectrum.shape[1]
    length = spectrum.shape[2]
    group_dev = filt.shape[1]
    a_real = spectrum[0].reshape(group_dev, chan_width // group_dev, length)
    a_imag = spectrum[1].reshape(group_dev, chan_width // group_dev, length)
    e_real = filt[0][:, None, :]
    e_imag = filt[1][:, None, :]
    first_col = lax.broadcasted_iota(jnp.int32, (1, 1, length), 2) == 0
    prod_real = jnp.where(first_col, a_real * e_real, a_real * e_real - a_imag * e_imag)
    prod_imag = jnp.where(first_col, a_imag * e_imag, a_real * e_imag + a_imag * e_real)
    return jnp.stack([prod_real.reshape(chan_width, length), prod_imag.reshape(chan_width, length)])


def filtered_sum(specs, filters):
    total = apply_filter(specs[0], filters[0])
    for spec, filt in zip(specs[1:], filters[1:]):
        total = total + apply_filter(spec, filt)
    return total


def body(queries, key_in, values_in, skip_gain, filter_tap_bank, lag_slot):
    length, chan_width = key_in.shape
    slots_dev = filter_tap_bank.shape[0]
    cycle_steps = lag_slot.shape[0]
    group_dev = filter_tap_bank.shape[2] // lax.axis_size("sub")
    n_ctx = lax.axis_size("ctx")
    sub_index = lax.axis_index("sub")
    mixed_input = key_in * values_in
    fwd_real, fwd_imag, inv_real, inv_imag = lax.optimization_barrier(tables(length))
    members = chan_width // group_dev
    n_sub = lax.axis_size("sub")
    received = []
    for offset in range(n_sub):
        wanted = lax.dynamic_slice_in_dim(
            filter_tap_bank, ((sub_index + offset) % n_sub) * group_dev, group_dev, 2
        )
        if offset:
            wanted = lax.ppermute(
                wanted, "sub", [(i, (i + offset) % n_sub) for i in range(n_sub)]
            )
        received.append(wanted)
    received = jnp.stack(received)
    pieces = []
    for cycle_step in range(cycle_steps):
        slot_index = lag_slot[cycle_step]
        owner = slot_index // slots_dev
        source = (sub_index - owner % n_sub) % n_sub
        held_piece = received[source, slot_index % slots_dev]
        pieces.append(from_root(held_piece, "ctx", owner // n_sub))
    filter_taps = jnp.concatenate(pieces, axis=1)
    filter_spec = jnp.stack(
        [
            jnp.einsum("pk,fp->kf", filter_taps, fwd_real, precision=HIGHEST),
            jnp.einsum("pk,fp->kf", filter_taps, fwd_imag, precision=HIGHEST),
        ]
    )
    col_sign = (
        1.0 - 2.0 * (lax.broadcasted_iota(jnp.int32, (1, length), 1) % 2).astype(jnp.float32)
    )[None]
    segment_spec = [
        filter_spec[:, cycle_step * group_dev : (cycle_step + 1) * group_dev]
        for cycle_step in range(cycle_steps)
    ]
    effective = [col_sign * segment_spec[0]]
    for cycle_step in range(1, cycle_steps):
        effective.append(segment_spec[cycle_step - 1] + col_sign * segment_spec[cycle_step])
    effective.append(segment_spec[cycle_steps - 1])

    last_raw = max(n_ctx - 2, 0)
    raw_rounds = min(cycle_steps, last_raw)
    part_terms = min(cycle_steps, raw_rounds + 1)
    chunks = CHUNKS if group_dev % CHUNKS == 0 else 1
    chunk_w = chan_width // chunks
    chunk_g = group_dev // chunks
    outs = []
    last_round = None
    partial = None
    sent = None
    for chunk in range(chunks):
        cols = slice(chunk * chunk_w, (chunk + 1) * chunk_w)
        filters = [e[:, chunk * chunk_g : (chunk + 1) * chunk_g] for e in effective]
        moving = mixed_input[:, cols]
        blocks = [moving]
        for step in range(1, raw_rounds + 1):
            route = [(k, k + 1) for k in range(step - 1, last_raw)]
            if step == raw_rounds and step > 1 and last_round is not None:
                moving, _ = lax.optimization_barrier((moving, last_round))
            moving = lax.ppermute(moving, "ctx", route)
            if step == raw_rounds and step > 1 and partial is not None:
                moving, _ = lax.optimization_barrier((moving, partial))
            blocks.append(moving)
        if raw_rounds > 1:
            last_round = blocks[-1]
        specs = [transform_rows(b, fwd_real, fwd_imag) for b in blocks]
        conv_out = inverse_rows(filtered_sum(specs, filters), inv_real, inv_imag)
        if n_ctx >= 2:
            part_specs = specs[:part_terms]
            if sent is not None:
                part_specs, _ = lax.optimization_barrier((part_specs, sent))
            partial = inverse_rows(
                filtered_sum(part_specs, filters[1 : part_terms + 1]), inv_real, inv_imag
            )
            sent = lax.ppermute(partial, "ctx", [(last_raw, last_raw + 1)])
            conv_out = conv_out + sent
        outs.append(conv_out)
    conv_all = jnp.concatenate(outs, axis=1) if chunks > 1 else outs[0]
    return queries * (conv_all + skip_gain[None, :] * mixed_input)


def solution(mesh):
    in_specs = (
        P(("groups", "ctx"), ("chan", "sub")),
        P(("groups", "ctx"), ("chan", "sub")),
        P(("groups", "ctx"), ("chan", "sub")),
        P(("chan", "sub")),
        P(("ctx", "sub"), None, "chan"),
        P(),
    )
    out_specs = P(("groups", "ctx"), ("chan", "sub"))
    return jax.shard_map(body, mesh=mesh, in_specs=in_specs, out_specs=out_specs, check_vma=False)
```

```python
import jax
import jax.numpy as jnp
from jax import lax
from jax.sharding import PartitionSpec as P

HIGHEST = lax.Precision.HIGHEST
DATA_PRECISION = lax.Precision.HIGH
CHUNKS = 4


def from_root(block, axis, owner):
    block = jnp.where(lax.axis_index(axis) == owner, block, jnp.zeros_like(block))
    return lax.psum(block, axis)


def tables(length):
    freq_rows = lax.broadcasted_iota(jnp.int32, (length, length), 0)
    place_cols = lax.broadcasted_iota(jnp.int32, (length, length), 1)
    angle = jnp.pi * (freq_rows * place_cols % (2 * length)).astype(jnp.float32) / length
    parity = 1.0 - 2.0 * (place_cols % 2).astype(jnp.float32)
    fwd_real = jnp.cos(angle)
    fwd_imag = jnp.where(freq_rows == 0, parity, -jnp.sin(angle))
    out_place = freq_rows + length
    back_angle = jnp.pi * (place_cols * out_place % (2 * length)).astype(jnp.float32) / length
    out_parity = 1.0 - 2.0 * (out_place % 2).astype(jnp.float32)
    inv_real = jnp.where(place_cols == 0, 1.0, 2.0 * jnp.cos(back_angle)) / (2 * length)
    inv_imag = jnp.where(place_cols == 0, out_parity, -2.0 * jnp.sin(back_angle)) / (2 * length)
    return (fwd_real, fwd_imag, inv_real, inv_imag)


def transform(block, fwd_real, fwd_imag, precision=DATA_PRECISION):
    return jnp.stack(
        [jnp.dot(fwd_real, block, precision=precision), jnp.dot(fwd_imag, block, precision=precision)]
    )


def transform_rows(block, fwd_real, fwd_imag):
    return jnp.stack(
        [
            jnp.einsum("pc,fp->cf", block, fwd_real, precision=DATA_PRECISION),
            jnp.einsum("pc,fp->cf", block, fwd_imag, precision=DATA_PRECISION),
        ]
    )


def inverse_rows(total, inv_real, inv_imag):
    return jnp.einsum("tf,cf->tc", inv_real, total[0], precision=DATA_PRECISION) + jnp.einsum(
        "tf,cf->tc", inv_imag, total[1], precision=DATA_PRECISION
    )


def apply_filter(spectrum, filt):
    chan_width = spectrum.shape[1]
    length = spectrum.shape[2]
    group_dev = filt.shape[1]
    a_real = spectrum[0].reshape(group_dev, chan_width // group_dev, length)
    a_imag = spectrum[1].reshape(group_dev, chan_width // group_dev, length)
    e_real = filt[0][:, None, :]
    e_imag = filt[1][:, None, :]
    first_col = lax.broadcasted_iota(jnp.int32, (1, 1, length), 2) == 0
    prod_real = jnp.where(first_col, a_real * e_real, a_real * e_real - a_imag * e_imag)
    prod_imag = jnp.where(first_col, a_imag * e_imag, a_real * e_imag + a_imag * e_real)
    return jnp.stack([prod_real.reshape(chan_width, length), prod_imag.reshape(chan_width, length)])


def filtered_sum(specs, filters):
    total = apply_filter(specs[0], filters[0])
    for spec, filt in zip(specs[1:], filters[1:]):
        total = total + apply_filter(spec, filt)
    return total


def body(queries, key_in, values_in, skip_gain, filter_tap_bank, lag_slot):
    length, chan_width = key_in.shape
    slots_dev = filter_tap_bank.shape[0]
    cycle_steps = lag_slot.shape[0]
    group_dev = filter_tap_bank.shape[2] // lax.axis_size("sub")
    n_ctx = lax.axis_size("ctx")
    sub_index = lax.axis_index("sub")
    fwd_real, fwd_imag, inv_real, inv_imag = lax.optimization_barrier(tables(length))
    members = chan_width // group_dev
    n_sub = lax.axis_size("sub")
    received = []
    for offset in range(n_sub):
        wanted = lax.dynamic_slice_in_dim(
            filter_tap_bank, ((sub_index + offset) % n_sub) * group_dev, group_dev, 2
        )
        if offset:
            wanted = lax.ppermute(
                wanted, "sub", [(i, (i + offset) % n_sub) for i in range(n_sub)]
            )
        received.append(wanted)
    received = jnp.stack(received)
    key_in, values_in, received = lax.optimization_barrier((key_in, values_in, received))
    mixed_input = key_in * values_in
    pieces = []
    for cycle_step in range(cycle_steps):
        slot_index = lag_slot[cycle_step]
        owner = slot_index // slots_dev
        source = (sub_index - owner % n_sub) % n_sub
        held_piece = received[source, slot_index % slots_dev]
        pieces.append(from_root(held_piece, "ctx", owner // n_sub))
    filter_taps = jnp.concatenate(pieces, axis=1)
    filter_spec = jnp.stack(
        [
            jnp.einsum("pk,fp->kf", filter_taps, fwd_real, precision=HIGHEST),
            jnp.einsum("pk,fp->kf", filter_taps, fwd_imag, precision=HIGHEST),
        ]
    )
    col_sign = (
        1.0 - 2.0 * (lax.broadcasted_iota(jnp.int32, (1, length), 1) % 2).astype(jnp.float32)
    )[None]
    segment_spec = [
        filter_spec[:, cycle_step * group_dev : (cycle_step + 1) * group_dev]
        for cycle_step in range(cycle_steps)
    ]
    effective = [col_sign * segment_spec[0]]
    for cycle_step in range(1, cycle_steps):
        effective.append(segment_spec[cycle_step - 1] + col_sign * segment_spec[cycle_step])
    effective.append(segment_spec[cycle_steps - 1])

    last_raw = max(n_ctx - 2, 0)
    raw_rounds = min(cycle_steps, last_raw)
    part_terms = min(cycle_steps, raw_rounds + 1)
    chunks = CHUNKS if group_dev % CHUNKS == 0 else 1
    chunk_w = chan_width // chunks
    chunk_g = group_dev // chunks
    outs = []
    last_round = None
    partial = None
    sent = None
    for chunk in range(chunks):
        cols = slice(chunk * chunk_w, (chunk + 1) * chunk_w)
        filters = [e[:, chunk * chunk_g : (chunk + 1) * chunk_g] for e in effective]
        moving = mixed_input[:, cols]
        blocks = [moving]
        for step in range(1, raw_rounds + 1):
            route = [(k, k + 1) for k in range(step - 1, last_raw)]
            if step == raw_rounds and step > 1 and last_round is not None:
                moving, _ = lax.optimization_barrier((moving, last_round))
            moving = lax.ppermute(moving, "ctx", route)
            if step == raw_rounds and step > 1 and partial is not None:
                moving, _ = lax.optimization_barrier((moving, partial))
            blocks.append(moving)
        if raw_rounds > 1:
            last_round = blocks[-1]
        specs = [transform_rows(b, fwd_real, fwd_imag) for b in blocks]
        conv_out = inverse_rows(filtered_sum(specs, filters), inv_real, inv_imag)
        if n_ctx >= 2:
            part_specs = specs[:part_terms]
            if sent is not None:
                part_specs, _ = lax.optimization_barrier((part_specs, sent))
            partial = inverse_rows(
                filtered_sum(part_specs, filters[1 : part_terms + 1]), inv_real, inv_imag
            )
            sent = lax.ppermute(partial, "ctx", [(last_raw, last_raw + 1)])
            conv_out = conv_out + sent
        outs.append(conv_out)
    conv_all = jnp.concatenate(outs, axis=1) if chunks > 1 else outs[0]
    return queries * (conv_all + skip_gain[None, :] * mixed_input)


def solution(mesh):
    in_specs = (
        P(("groups", "ctx"), ("chan", "sub")),
        P(("groups", "ctx"), ("chan", "sub")),
        P(("groups", "ctx"), ("chan", "sub")),
        P(("chan", "sub")),
        P(("ctx", "sub"), None, "chan"),
        P(),
    )
    out_specs = P(("groups", "ctx"), ("chan", "sub"))
    return jax.shard_map(body, mesh=mesh, in_specs=in_specs, out_specs=out_specs, check_vma=False)
```

```python
import jax
import jax.numpy as jnp
from jax import lax
from jax.sharding import PartitionSpec as P

HIGHEST = lax.Precision.HIGHEST
DATA_PRECISION = lax.Precision.HIGH
CHUNKS = 4


def from_root(block, axis, owner):
    block = jnp.where(lax.axis_index(axis) == owner, block, jnp.zeros_like(block))
    return lax.psum(block, axis)


def tables(length):
    freq_rows = lax.broadcasted_iota(jnp.int32, (length, length), 0)
    place_cols = lax.broadcasted_iota(jnp.int32, (length, length), 1)
    angle = jnp.pi * (freq_rows * place_cols % (2 * length)).astype(jnp.float32) / length
    parity = 1.0 - 2.0 * (place_cols % 2).astype(jnp.float32)
    fwd_real = jnp.cos(angle)
    fwd_imag = jnp.where(freq_rows == 0, parity, -jnp.sin(angle))
    out_place = freq_rows + length
    back_angle = jnp.pi * (place_cols * out_place % (2 * length)).astype(jnp.float32) / length
    out_parity = 1.0 - 2.0 * (out_place % 2).astype(jnp.float32)
    inv_real = jnp.where(place_cols == 0, 1.0, 2.0 * jnp.cos(back_angle)) / (2 * length)
    inv_imag = jnp.where(place_cols == 0, out_parity, -2.0 * jnp.sin(back_angle)) / (2 * length)
    return (fwd_real, fwd_imag, inv_real, inv_imag)


def transform(block, fwd_real, fwd_imag, precision=DATA_PRECISION):
    return jnp.stack(
        [jnp.dot(fwd_real, block, precision=precision), jnp.dot(fwd_imag, block, precision=precision)]
    )


def transform_rows(block, fwd_real, fwd_imag):
    return jnp.stack(
        [
            jnp.einsum("pc,fp->cf", block, fwd_real, precision=DATA_PRECISION),
            jnp.einsum("pc,fp->cf", block, fwd_imag, precision=DATA_PRECISION),
        ]
    )


def inverse_rows(total, inv_real, inv_imag):
    return jnp.einsum("tf,cf->tc", inv_real, total[0], precision=DATA_PRECISION) + jnp.einsum(
        "tf,cf->tc", inv_imag, total[1], precision=DATA_PRECISION
    )


def apply_filter(spectrum, filt):
    chan_width = spectrum.shape[1]
    length = spectrum.shape[2]
    group_dev = filt.shape[1]
    a_real = spectrum[0].reshape(group_dev, chan_width // group_dev, length)
    a_imag = spectrum[1].reshape(group_dev, chan_width // group_dev, length)
    e_real = filt[0][:, None, :]
    e_imag = filt[1][:, None, :]
    first_col = lax.broadcasted_iota(jnp.int32, (1, 1, length), 2) == 0
    prod_real = jnp.where(first_col, a_real * e_real, a_real * e_real - a_imag * e_imag)
    prod_imag = jnp.where(first_col, a_imag * e_imag, a_real * e_imag + a_imag * e_real)
    return jnp.stack([prod_real.reshape(chan_width, length), prod_imag.reshape(chan_width, length)])


def filtered_sum(specs, filters):
    total = apply_filter(specs[0], filters[0])
    for spec, filt in zip(specs[1:], filters[1:]):
        total = total + apply_filter(spec, filt)
    return total


def body(queries, key_in, values_in, skip_gain, filter_tap_bank, lag_slot):
    length, chan_width = key_in.shape
    slots_dev = filter_tap_bank.shape[0]
    cycle_steps = lag_slot.shape[0]
    group_dev = filter_tap_bank.shape[2] // lax.axis_size("sub")
    n_ctx = lax.axis_size("ctx")
    sub_index = lax.axis_index("sub")
    mixed_input = key_in * values_in
    fwd_real, fwd_imag, inv_real, inv_imag = lax.optimization_barrier(tables(length))
    members = chan_width // group_dev
    n_sub = lax.axis_size("sub")
    received = []
    for offset in range(n_sub):
        wanted = lax.dynamic_slice_in_dim(
            filter_tap_bank, ((sub_index + offset) % n_sub) * group_dev, group_dev, 2
        )
        if offset:
            wanted = lax.ppermute(
                wanted, "sub", [(i, (i + offset) % n_sub) for i in range(n_sub)]
            )
        received.append(wanted)
    received = jnp.stack(received)
    pieces = []
    for cycle_step in range(cycle_steps):
        slot_index = lag_slot[cycle_step]
        owner = slot_index // slots_dev
        source = (sub_index - owner % n_sub) % n_sub
        held_piece = received[source, slot_index % slots_dev]
        pieces.append(from_root(held_piece, "ctx", owner // n_sub))
    filter_taps = jnp.concatenate(pieces, axis=1)
    filter_spec = jnp.stack(
        [
            jnp.einsum("pk,fp->kf", filter_taps, fwd_real, precision=HIGHEST),
            jnp.einsum("pk,fp->kf", filter_taps, fwd_imag, precision=HIGHEST),
        ]
    )
    col_sign = (
        1.0 - 2.0 * (lax.broadcasted_iota(jnp.int32, (1, length), 1) % 2).astype(jnp.float32)
    )[None]
    segment_spec = [
        filter_spec[:, cycle_step * group_dev : (cycle_step + 1) * group_dev]
        for cycle_step in range(cycle_steps)
    ]
    effective = [col_sign * segment_spec[0]]
    for cycle_step in range(1, cycle_steps):
        effective.append(segment_spec[cycle_step - 1] + col_sign * segment_spec[cycle_step])
    effective.append(segment_spec[cycle_steps - 1])

    last_raw = max(n_ctx - 2, 0)
    raw_rounds = min(cycle_steps, last_raw)
    part_terms = min(cycle_steps, raw_rounds + 1)
    chunks = CHUNKS if group_dev % CHUNKS == 0 else 1
    chunk_w = chan_width // chunks
    chunk_g = group_dev // chunks
    first_round = None
    if raw_rounds:
        first_round = lax.ppermute(mixed_input, "ctx", [(k, k + 1) for k in range(0, last_raw)])
    outs = []
    last_round = None
    partial = None
    sent = None
    for chunk in range(chunks):
        cols = slice(chunk * chunk_w, (chunk + 1) * chunk_w)
        filters = [e[:, chunk * chunk_g : (chunk + 1) * chunk_g] for e in effective]
        moving = mixed_input[:, cols]
        blocks = [moving]
        for step in range(1, raw_rounds + 1):
            route = [(k, k + 1) for k in range(step - 1, last_raw)]
            if step == raw_rounds and step > 1 and last_round is not None:
                moving, _ = lax.optimization_barrier((moving, last_round))
            if step == 1:
                moving = first_round[:, cols]
            else:
                moving = lax.ppermute(moving, "ctx", route)
            if step == raw_rounds and step > 1 and partial is not None:
                moving, _ = lax.optimization_barrier((moving, partial))
            blocks.append(moving)
        if raw_rounds > 1:
            last_round = blocks[-1]
        specs = [transform_rows(b, fwd_real, fwd_imag) for b in blocks]
        conv_out = inverse_rows(filtered_sum(specs, filters), inv_real, inv_imag)
        if n_ctx >= 2:
            part_specs = specs[:part_terms]
            if sent is not None:
                part_specs, _ = lax.optimization_barrier((part_specs, sent))
            partial = inverse_rows(
                filtered_sum(part_specs, filters[1 : part_terms + 1]), inv_real, inv_imag
            )
            sent = lax.ppermute(partial, "ctx", [(last_raw, last_raw + 1)])
            conv_out = conv_out + sent
        outs.append(conv_out)
    conv_all = jnp.concatenate(outs, axis=1) if chunks > 1 else outs[0]
    return queries * (conv_all + skip_gain[None, :] * mixed_input)


def solution(mesh):
    in_specs = (
        P(("groups", "ctx"), ("chan", "sub")),
        P(("groups", "ctx"), ("chan", "sub")),
        P(("groups", "ctx"), ("chan", "sub")),
        P(("chan", "sub")),
        P(("ctx", "sub"), None, "chan"),
        P(),
    )
    out_specs = P(("groups", "ctx"), ("chan", "sub"))
    return jax.shard_map(body, mesh=mesh, in_specs=in_specs, out_specs=out_specs, check_vma=False)
```

```python
import jax
import jax.numpy as jnp
from jax import lax
from jax.sharding import PartitionSpec as P

HIGHEST = lax.Precision.HIGHEST
DATA_PRECISION = lax.Precision.HIGH
CHUNKS = 4


def from_root(block, axis, owner):
    block = jnp.where(lax.axis_index(axis) == owner, block, jnp.zeros_like(block))
    return lax.psum(block, axis)


def tables(length):
    freq_rows = lax.broadcasted_iota(jnp.int32, (length, length), 0)
    place_cols = lax.broadcasted_iota(jnp.int32, (length, length), 1)
    angle = jnp.pi * (freq_rows * place_cols % (2 * length)).astype(jnp.float32) / length
    parity = 1.0 - 2.0 * (place_cols % 2).astype(jnp.float32)
    fwd_real = jnp.cos(angle)
    fwd_imag = jnp.where(freq_rows == 0, parity, -jnp.sin(angle))
    out_place = freq_rows + length
    back_angle = jnp.pi * (place_cols * out_place % (2 * length)).astype(jnp.float32) / length
    out_parity = 1.0 - 2.0 * (out_place % 2).astype(jnp.float32)
    inv_real = jnp.where(place_cols == 0, 1.0, 2.0 * jnp.cos(back_angle)) / (2 * length)
    inv_imag = jnp.where(place_cols == 0, out_parity, -2.0 * jnp.sin(back_angle)) / (2 * length)
    return (fwd_real, fwd_imag, inv_real, inv_imag)


def transform(block, fwd_real, fwd_imag, precision=DATA_PRECISION):
    return jnp.stack(
        [jnp.dot(fwd_real, block, precision=precision), jnp.dot(fwd_imag, block, precision=precision)]
    )


def transform_rows(block, fwd_real, fwd_imag):
    return jnp.stack(
        [
            jnp.einsum("pc,fp->cf", block, fwd_real, precision=DATA_PRECISION),
            jnp.einsum("pc,fp->cf", block, fwd_imag, precision=DATA_PRECISION),
        ]
    )


def inverse_rows(total, inv_real, inv_imag):
    return jnp.einsum("tf,cf->tc", inv_real, total[0], precision=DATA_PRECISION) + jnp.einsum(
        "tf,cf->tc", inv_imag, total[1], precision=DATA_PRECISION
    )


def apply_filter(spectrum, filt):
    chan_width = spectrum.shape[1]
    length = spectrum.shape[2]
    group_dev = filt.shape[1]
    a_real = spectrum[0].reshape(group_dev, chan_width // group_dev, length)
    a_imag = spectrum[1].reshape(group_dev, chan_width // group_dev, length)
    e_real = filt[0][:, None, :]
    e_imag = filt[1][:, None, :]
    first_col = lax.broadcasted_iota(jnp.int32, (1, 1, length), 2) == 0
    prod_real = jnp.where(first_col, a_real * e_real, a_real * e_real - a_imag * e_imag)
    prod_imag = jnp.where(first_col, a_imag * e_imag, a_real * e_imag + a_imag * e_real)
    return jnp.stack([prod_real.reshape(chan_width, length), prod_imag.reshape(chan_width, length)])


def filtered_sum(specs, filters):
    total = apply_filter(specs[0], filters[0])
    for spec, filt in zip(specs[1:], filters[1:]):
        total = total + apply_filter(spec, filt)
    return total


def body(queries, key_in, values_in, skip_gain, filter_tap_bank, lag_slot):
    length, chan_width = key_in.shape
    slots_dev = filter_tap_bank.shape[0]
    cycle_steps = lag_slot.shape[0]
    group_dev = filter_tap_bank.shape[2] // lax.axis_size("sub")
    n_ctx = lax.axis_size("ctx")
    sub_index = lax.axis_index("sub")
    mixed_input = key_in * values_in
    fwd_real, fwd_imag, inv_real, inv_imag = lax.optimization_barrier(tables(length))
    members = chan_width // group_dev
    n_sub = lax.axis_size("sub")
    received = []
    for offset in range(n_sub):
        wanted = lax.dynamic_slice_in_dim(
            filter_tap_bank, ((sub_index + offset) % n_sub) * group_dev, group_dev, 2
        )
        if offset:
            wanted = lax.ppermute(
                wanted, "sub", [(i, (i + offset) % n_sub) for i in range(n_sub)]
            )
        received.append(wanted)
    received = jnp.stack(received)
    key_in, values_in, received = lax.optimization_barrier((key_in, values_in, received))
    mixed_input = key_in * values_in
    pieces = []
    for cycle_step in range(cycle_steps):
        slot_index = lag_slot[cycle_step]
        owner = slot_index // slots_dev
        source = (sub_index - owner % n_sub) % n_sub
        held_piece = received[source, slot_index % slots_dev]
        pieces.append(from_root(held_piece, "ctx", owner // n_sub))
    filter_taps = jnp.concatenate(pieces, axis=1)
    filter_spec = jnp.stack(
        [
            jnp.einsum("pk,fp->kf", filter_taps, fwd_real, precision=HIGHEST),
            jnp.einsum("pk,fp->kf", filter_taps, fwd_imag, precision=HIGHEST),
        ]
    )
    col_sign = (
        1.0 - 2.0 * (lax.broadcasted_iota(jnp.int32, (1, length), 1) % 2).astype(jnp.float32)
    )[None]
    segment_spec = [
        filter_spec[:, cycle_step * group_dev : (cycle_step + 1) * group_dev]
        for cycle_step in range(cycle_steps)
    ]
    effective = [col_sign * segment_spec[0]]
    for cycle_step in range(1, cycle_steps):
        effective.append(segment_spec[cycle_step - 1] + col_sign * segment_spec[cycle_step])
    effective.append(segment_spec[cycle_steps - 1])

    last_raw = max(n_ctx - 2, 0)
    raw_rounds = min(cycle_steps, last_raw)
    part_terms = min(cycle_steps, raw_rounds + 1)
    chunks = CHUNKS if group_dev % CHUNKS == 0 else 1
    chunk_w = chan_width // chunks
    chunk_g = group_dev // chunks
    first_round = None
    if raw_rounds:
        first_round = lax.ppermute(mixed_input, "ctx", [(k, k + 1) for k in range(0, last_raw)])
    outs = []
    last_round = None
    partial = None
    sent = None
    for chunk in range(chunks):
        cols = slice(chunk * chunk_w, (chunk + 1) * chunk_w)
        filters = [e[:, chunk * chunk_g : (chunk + 1) * chunk_g] for e in effective]
        moving = mixed_input[:, cols]
        blocks = [moving]
        for step in range(1, raw_rounds + 1):
            route = [(k, k + 1) for k in range(step - 1, last_raw)]
            if step == raw_rounds and step > 1 and last_round is not None:
                moving, _ = lax.optimization_barrier((moving, last_round))
            if step == 1:
                moving = first_round[:, cols]
            else:
                moving = lax.ppermute(moving, "ctx", route)
            if step == raw_rounds and step > 1 and partial is not None:
                moving, _ = lax.optimization_barrier((moving, partial))
            blocks.append(moving)
        if raw_rounds > 1:
            last_round = blocks[-1]
        specs = [transform_rows(b, fwd_real, fwd_imag) for b in blocks]
        conv_out = inverse_rows(filtered_sum(specs, filters), inv_real, inv_imag)
        if n_ctx >= 2:
            part_specs = specs[:part_terms]
            if sent is not None:
                part_specs, _ = lax.optimization_barrier((part_specs, sent))
            partial = inverse_rows(
                filtered_sum(part_specs, filters[1 : part_terms + 1]), inv_real, inv_imag
            )
            sent = lax.ppermute(partial, "ctx", [(last_raw, last_raw + 1)])
            conv_out = conv_out + sent
        outs.append(conv_out)
    conv_all = jnp.concatenate(outs, axis=1) if chunks > 1 else outs[0]
    return queries * (conv_all + skip_gain[None, :] * mixed_input)


def solution(mesh):
    in_specs = (
        P(("groups", "ctx"), ("chan", "sub")),
        P(("groups", "ctx"), ("chan", "sub")),
        P(("groups", "ctx"), ("chan", "sub")),
        P(("chan", "sub")),
        P(("ctx", "sub"), None, "chan"),
        P(),
    )
    out_specs = P(("groups", "ctx"), ("chan", "sub"))
    return jax.shard_map(body, mesh=mesh, in_specs=in_specs, out_specs=out_specs, check_vma=False)
```

```python
import jax
import jax.numpy as jnp
from jax import lax
from jax.sharding import PartitionSpec as P

HIGHEST = lax.Precision.HIGHEST
DATA_PRECISION = lax.Precision.HIGH
CHUNKS = 8


def from_root(block, axis, owner):
    block = jnp.where(lax.axis_index(axis) == owner, block, jnp.zeros_like(block))
    return lax.psum(block, axis)


def tables(length):
    freq_rows = lax.broadcasted_iota(jnp.int32, (length, length), 0)
    place_cols = lax.broadcasted_iota(jnp.int32, (length, length), 1)
    angle = jnp.pi * (freq_rows * place_cols % (2 * length)).astype(jnp.float32) / length
    parity = 1.0 - 2.0 * (place_cols % 2).astype(jnp.float32)
    fwd_real = jnp.cos(angle)
    fwd_imag = jnp.where(freq_rows == 0, parity, -jnp.sin(angle))
    out_place = freq_rows + length
    back_angle = jnp.pi * (place_cols * out_place % (2 * length)).astype(jnp.float32) / length
    out_parity = 1.0 - 2.0 * (out_place % 2).astype(jnp.float32)
    inv_real = jnp.where(place_cols == 0, 1.0, 2.0 * jnp.cos(back_angle)) / (2 * length)
    inv_imag = jnp.where(place_cols == 0, out_parity, -2.0 * jnp.sin(back_angle)) / (2 * length)
    return (fwd_real, fwd_imag, inv_real, inv_imag)


def transform(block, fwd_real, fwd_imag, precision=DATA_PRECISION):
    return jnp.stack(
        [jnp.dot(fwd_real, block, precision=precision), jnp.dot(fwd_imag, block, precision=precision)]
    )


def transform_rows(block, fwd_real, fwd_imag):
    return jnp.stack(
        [
            jnp.einsum("pc,fp->cf", block, fwd_real, precision=DATA_PRECISION),
            jnp.einsum("pc,fp->cf", block, fwd_imag, precision=DATA_PRECISION),
        ]
    )


def inverse_rows(total, inv_real, inv_imag):
    return jnp.einsum("tf,cf->tc", inv_real, total[0], precision=DATA_PRECISION) + jnp.einsum(
        "tf,cf->tc", inv_imag, total[1], precision=DATA_PRECISION
    )


def apply_filter(spectrum, filt):
    chan_width = spectrum.shape[1]
    length = spectrum.shape[2]
    group_dev = filt.shape[1]
    a_real = spectrum[0].reshape(group_dev, chan_width // group_dev, length)
    a_imag = spectrum[1].reshape(group_dev, chan_width // group_dev, length)
    e_real = filt[0][:, None, :]
    e_imag = filt[1][:, None, :]
    first_col = lax.broadcasted_iota(jnp.int32, (1, 1, length), 2) == 0
    prod_real = jnp.where(first_col, a_real * e_real, a_real * e_real - a_imag * e_imag)
    prod_imag = jnp.where(first_col, a_imag * e_imag, a_real * e_imag + a_imag * e_real)
    return jnp.stack([prod_real.reshape(chan_width, length), prod_imag.reshape(chan_width, length)])


def filtered_sum(specs, filters):
    total = apply_filter(specs[0], filters[0])
    for spec, filt in zip(specs[1:], filters[1:]):
        total = total + apply_filter(spec, filt)
    return total


def body(queries, key_in, values_in, skip_gain, filter_tap_bank, lag_slot):
    length, chan_width = key_in.shape
    slots_dev = filter_tap_bank.shape[0]
    cycle_steps = lag_slot.shape[0]
    group_dev = filter_tap_bank.shape[2] // lax.axis_size("sub")
    n_ctx = lax.axis_size("ctx")
    sub_index = lax.axis_index("sub")
    mixed_input = key_in * values_in
    fwd_real, fwd_imag, inv_real, inv_imag = lax.optimization_barrier(tables(length))
    members = chan_width // group_dev
    n_sub = lax.axis_size("sub")
    received = []
    for offset in range(n_sub):
        wanted = lax.dynamic_slice_in_dim(
            filter_tap_bank, ((sub_index + offset) % n_sub) * group_dev, group_dev, 2
        )
        if offset:
            wanted = lax.ppermute(
                wanted, "sub", [(i, (i + offset) % n_sub) for i in range(n_sub)]
            )
        received.append(wanted)
    received = jnp.stack(received)
    pieces = []
    for cycle_step in range(cycle_steps):
        slot_index = lag_slot[cycle_step]
        owner = slot_index // slots_dev
        source = (sub_index - owner % n_sub) % n_sub
        held_piece = received[source, slot_index % slots_dev]
        pieces.append(from_root(held_piece, "ctx", owner // n_sub))
    filter_taps = jnp.concatenate(pieces, axis=1)
    filter_spec = jnp.stack(
        [
            jnp.einsum("pk,fp->kf", filter_taps, fwd_real, precision=HIGHEST),
            jnp.einsum("pk,fp->kf", filter_taps, fwd_imag, precision=HIGHEST),
        ]
    )
    col_sign = (
        1.0 - 2.0 * (lax.broadcasted_iota(jnp.int32, (1, length), 1) % 2).astype(jnp.float32)
    )[None]
    segment_spec = [
        filter_spec[:, cycle_step * group_dev : (cycle_step + 1) * group_dev]
        for cycle_step in range(cycle_steps)
    ]
    effective = [col_sign * segment_spec[0]]
    for cycle_step in range(1, cycle_steps):
        effective.append(segment_spec[cycle_step - 1] + col_sign * segment_spec[cycle_step])
    effective.append(segment_spec[cycle_steps - 1])

    last_raw = max(n_ctx - 2, 0)
    raw_rounds = min(cycle_steps, last_raw)
    part_terms = min(cycle_steps, raw_rounds + 1)
    chunks = CHUNKS if group_dev % CHUNKS == 0 else 1
    chunk_w = chan_width // chunks
    chunk_g = group_dev // chunks
    first_round = None
    if raw_rounds:
        first_round = lax.ppermute(mixed_input, "ctx", [(k, k + 1) for k in range(0, last_raw)])
    outs = []
    last_round = None
    partial = None
    sent = None
    for chunk in range(chunks):
        cols = slice(chunk * chunk_w, (chunk + 1) * chunk_w)
        filters = [e[:, chunk * chunk_g : (chunk + 1) * chunk_g] for e in effective]
        moving = mixed_input[:, cols]
        blocks = [moving]
        for step in range(1, raw_rounds + 1):
            route = [(k, k + 1) for k in range(step - 1, last_raw)]
            if step == raw_rounds and step > 1 and last_round is not None:
                moving, _ = lax.optimization_barrier((moving, last_round))
            if step == 1:
                moving = first_round[:, cols]
            else:
                moving = lax.ppermute(moving, "ctx", route)
            if step == raw_rounds and step > 1 and partial is not None:
                moving, _ = lax.optimization_barrier((moving, partial))
            blocks.append(moving)
        if raw_rounds > 1:
            last_round = blocks[-1]
        specs = [transform_rows(b, fwd_real, fwd_imag) for b in blocks]
        conv_out = inverse_rows(filtered_sum(specs, filters), inv_real, inv_imag)
        if n_ctx >= 2:
            part_specs = specs[:part_terms]
            if sent is not None:
                part_specs, _ = lax.optimization_barrier((part_specs, sent))
            partial = inverse_rows(
                filtered_sum(part_specs, filters[1 : part_terms + 1]), inv_real, inv_imag
            )
            sent = lax.ppermute(partial, "ctx", [(last_raw, last_raw + 1)])
            conv_out = conv_out + sent
        outs.append(conv_out)
    conv_all = jnp.concatenate(outs, axis=1) if chunks > 1 else outs[0]
    return queries * (conv_all + skip_gain[None, :] * mixed_input)


def solution(mesh):
    in_specs = (
        P(("groups", "ctx"), ("chan", "sub")),
        P(("groups", "ctx"), ("chan", "sub")),
        P(("groups", "ctx"), ("chan", "sub")),
        P(("chan", "sub")),
        P(("ctx", "sub"), None, "chan"),
        P(),
    )
    out_specs = P(("groups", "ctx"), ("chan", "sub"))
    return jax.shard_map(body, mesh=mesh, in_specs=in_specs, out_specs=out_specs, check_vma=False)
```

```python
import jax
import jax.numpy as jnp
from jax import lax
from jax.sharding import PartitionSpec as P

HIGHEST = lax.Precision.HIGHEST
DATA_PRECISION = lax.Precision.HIGH
CHUNKS = 2


def from_root(block, axis, owner):
    block = jnp.where(lax.axis_index(axis) == owner, block, jnp.zeros_like(block))
    return lax.psum(block, axis)


def tables(length):
    freq_rows = lax.broadcasted_iota(jnp.int32, (length, length), 0)
    place_cols = lax.broadcasted_iota(jnp.int32, (length, length), 1)
    angle = jnp.pi * (freq_rows * place_cols % (2 * length)).astype(jnp.float32) / length
    parity = 1.0 - 2.0 * (place_cols % 2).astype(jnp.float32)
    fwd_real = jnp.cos(angle)
    fwd_imag = jnp.where(freq_rows == 0, parity, -jnp.sin(angle))
    out_place = freq_rows + length
    back_angle = jnp.pi * (place_cols * out_place % (2 * length)).astype(jnp.float32) / length
    out_parity = 1.0 - 2.0 * (out_place % 2).astype(jnp.float32)
    inv_real = jnp.where(place_cols == 0, 1.0, 2.0 * jnp.cos(back_angle)) / (2 * length)
    inv_imag = jnp.where(place_cols == 0, out_parity, -2.0 * jnp.sin(back_angle)) / (2 * length)
    return (fwd_real, fwd_imag, inv_real, inv_imag)


def transform(block, fwd_real, fwd_imag, precision=DATA_PRECISION):
    return jnp.stack(
        [jnp.dot(fwd_real, block, precision=precision), jnp.dot(fwd_imag, block, precision=precision)]
    )


def transform_rows(block, fwd_real, fwd_imag):
    return jnp.stack(
        [
            jnp.einsum("pc,fp->cf", block, fwd_real, precision=DATA_PRECISION),
            jnp.einsum("pc,fp->cf", block, fwd_imag, precision=DATA_PRECISION),
        ]
    )


def inverse_rows(total, inv_real, inv_imag):
    return jnp.einsum("tf,cf->tc", inv_real, total[0], precision=DATA_PRECISION) + jnp.einsum(
        "tf,cf->tc", inv_imag, total[1], precision=DATA_PRECISION
    )


def apply_filter(spectrum, filt):
    chan_width = spectrum.shape[1]
    length = spectrum.shape[2]
    group_dev = filt.shape[1]
    a_real = spectrum[0].reshape(group_dev, chan_width // group_dev, length)
    a_imag = spectrum[1].reshape(group_dev, chan_width // group_dev, length)
    e_real = filt[0][:, None, :]
    e_imag = filt[1][:, None, :]
    first_col = lax.broadcasted_iota(jnp.int32, (1, 1, length), 2) == 0
    prod_real = jnp.where(first_col, a_real * e_real, a_real * e_real - a_imag * e_imag)
    prod_imag = jnp.where(first_col, a_imag * e_imag, a_real * e_imag + a_imag * e_real)
    return jnp.stack([prod_real.reshape(chan_width, length), prod_imag.reshape(chan_width, length)])


def filtered_sum(specs, filters):
    total = apply_filter(specs[0], filters[0])
    for spec, filt in zip(specs[1:], filters[1:]):
        total = total + apply_filter(spec, filt)
    return total


def body(queries, key_in, values_in, skip_gain, filter_tap_bank, lag_slot):
    length, chan_width = key_in.shape
    slots_dev = filter_tap_bank.shape[0]
    cycle_steps = lag_slot.shape[0]
    group_dev = filter_tap_bank.shape[2] // lax.axis_size("sub")
    n_ctx = lax.axis_size("ctx")
    sub_index = lax.axis_index("sub")
    mixed_input = key_in * values_in
    fwd_real, fwd_imag, inv_real, inv_imag = lax.optimization_barrier(tables(length))
    members = chan_width // group_dev
    n_sub = lax.axis_size("sub")
    received = []
    for offset in range(n_sub):
        wanted = lax.dynamic_slice_in_dim(
            filter_tap_bank, ((sub_index + offset) % n_sub) * group_dev, group_dev, 2
        )
        if offset:
            wanted = lax.ppermute(
                wanted, "sub", [(i, (i + offset) % n_sub) for i in range(n_sub)]
            )
        received.append(wanted)
    received = jnp.stack(received)
    pieces = []
    for cycle_step in range(cycle_steps):
        slot_index = lag_slot[cycle_step]
        owner = slot_index // slots_dev
        source = (sub_index - owner % n_sub) % n_sub
        held_piece = received[source, slot_index % slots_dev]
        pieces.append(from_root(held_piece, "ctx", owner // n_sub))
    filter_taps = jnp.concatenate(pieces, axis=1)
    filter_spec = jnp.stack(
        [
            jnp.einsum("pk,fp->kf", filter_taps, fwd_real, precision=HIGHEST),
            jnp.einsum("pk,fp->kf", filter_taps, fwd_imag, precision=HIGHEST),
        ]
    )
    col_sign = (
        1.0 - 2.0 * (lax.broadcasted_iota(jnp.int32, (1, length), 1) % 2).astype(jnp.float32)
    )[None]
    segment_spec = [
        filter_spec[:, cycle_step * group_dev : (cycle_step + 1) * group_dev]
        for cycle_step in range(cycle_steps)
    ]
    effective = [col_sign * segment_spec[0]]
    for cycle_step in range(1, cycle_steps):
        effective.append(segment_spec[cycle_step - 1] + col_sign * segment_spec[cycle_step])
    effective.append(segment_spec[cycle_steps - 1])

    last_raw = max(n_ctx - 2, 0)
    raw_rounds = min(cycle_steps, last_raw)
    part_terms = min(cycle_steps, raw_rounds + 1)
    chunks = CHUNKS if group_dev % CHUNKS == 0 else 1
    chunk_w = chan_width // chunks
    chunk_g = group_dev // chunks
    first_round = None
    if raw_rounds:
        first_round = lax.ppermute(mixed_input, "ctx", [(k, k + 1) for k in range(0, last_raw)])
    outs = []
    last_round = None
    partial = None
    sent = None
    for chunk in range(chunks):
        cols = slice(chunk * chunk_w, (chunk + 1) * chunk_w)
        filters = [e[:, chunk * chunk_g : (chunk + 1) * chunk_g] for e in effective]
        moving = mixed_input[:, cols]
        blocks = [moving]
        for step in range(1, raw_rounds + 1):
            route = [(k, k + 1) for k in range(step - 1, last_raw)]
            if step == raw_rounds and step > 1 and last_round is not None:
                moving, _ = lax.optimization_barrier((moving, last_round))
            if step == 1:
                moving = first_round[:, cols]
            else:
                moving = lax.ppermute(moving, "ctx", route)
            if step == raw_rounds and step > 1 and partial is not None:
                moving, _ = lax.optimization_barrier((moving, partial))
            blocks.append(moving)
        if raw_rounds > 1:
            last_round = blocks[-1]
        specs = [transform_rows(b, fwd_real, fwd_imag) for b in blocks]
        conv_out = inverse_rows(filtered_sum(specs, filters), inv_real, inv_imag)
        if n_ctx >= 2:
            part_specs = specs[:part_terms]
            if sent is not None:
                part_specs, _ = lax.optimization_barrier((part_specs, sent))
            partial = inverse_rows(
                filtered_sum(part_specs, filters[1 : part_terms + 1]), inv_real, inv_imag
            )
            sent = lax.ppermute(partial, "ctx", [(last_raw, last_raw + 1)])
            conv_out = conv_out + sent
        outs.append(conv_out)
    conv_all = jnp.concatenate(outs, axis=1) if chunks > 1 else outs[0]
    return queries * (conv_all + skip_gain[None, :] * mixed_input)


def solution(mesh):
    in_specs = (
        P(("groups", "ctx"), ("chan", "sub")),
        P(("groups", "ctx"), ("chan", "sub")),
        P(("groups", "ctx"), ("chan", "sub")),
        P(("chan", "sub")),
        P(("ctx", "sub"), None, "chan"),
        P(),
    )
    out_specs = P(("groups", "ctx"), ("chan", "sub"))
    return jax.shard_map(body, mesh=mesh, in_specs=in_specs, out_specs=out_specs, check_vma=False)
```
